128 devices in a mesh: chan: 32 (over x, y_lo, z), blk: 4 (over y_hi, core).
Axes of the slice: x: 4, y: 4 (y_hi: 2, y_lo: 2; y = y_hi * 2 + y_lo), z: 4, core: 2. Of those that a mesh axis runs over, the one named last changes fastest.
Arguments:
- voltages: int32 [2048, 134656], P(('chan', 'blk')), may hold values from -128 to 127
- flags: int32 [2048], P(('chan', 'blk')), may hold values 0 or 1
- model_amp: float32 [128, 2048], P('chan'), may hold values from 0.04 to 0.4
- model_phase: float32 [128, 2048], P('chan'), may hold values from -3.140625 to 3.140625
Outputs:
- visibility: bfloat16 [2, 128, 2048, 2048], P(None, 'chan', 'blk')
- gains: float32 [2, 128, 2048], P(None, None, ('chan', 'blk'))
The draws below stay inside these ranges and needn't reach their ends.
All inputs are finite; a program needn't handle non-finite values. No bound on the sum of `flags` on one device may be relied on, other than what follows from the above.
Results may differ from the reference program's by a relative error of at most 0.0091.
Values may be sent and summed in bfloat16 or wider, within the bound.
No kernel may reach another device: no remote copies, remote signals or barrier semaphores. Data moves between devices by JAX's collectives and lax.ppermute only.
A program may use at most 256 MiB of HBM per device.

```python
import math
import jax
import jax.numpy as jnp
from jax import lax

INPUTS = 2048
CHANS = 128
FRAME = 512
TAPS = 8
BAND_START = 64
SPECTRA = 256
ITERS = 10
SAMPLES = 134656


def set_ends(entries, stream_key, smallest, high):
    shape = entries.shape
    spot = [jax.random.randint(jax.random.fold_in(stream_key, axis), (), 0, shape[axis]) for axis in range(len(shape))]
    entries = entries.at[tuple(spot)].set(smallest)
    longest = shape.index(max(shape))
    spot[longest] = (spot[longest] + 1) % shape[longest]
    return entries.at[tuple(spot)].set(high)


def block_scale(own_key, dims, cuts, low, high):
    def one(position, shards_of):
        draws = jax.random.uniform(jax.random.fold_in(jax.random.fold_in(own_key, 6), position), (shards_of,), jnp.float32, low / len(cuts), high / len(cuts))
        return jnp.repeat(jnp.exp(draws), dims[position] // shards_of).reshape((-1,) + (1,) * (len(dims) - position - 1))

    gain = one(*cuts[0])
    for cut in cuts[1:]:
        gain = gain * one(*cut)
    return gain


def setup_inputs(seed: int = 0) -> dict:
    keys = jax.random.split(jax.random.key(seed), 5)
    voltages = set_ends(jax.random.randint(keys[0], (INPUTS, SAMPLES), -128, 128), jax.random.fold_in(keys[0], 1), -128, 127).astype(jnp.int32)
    flags = set_ends((jax.random.randint(keys[1], (INPUTS,), 0, 16) < 1).astype(jnp.int32), jax.random.fold_in(keys[1], 1), 0, 1)
    model_amp = jnp.clip(jnp.exp(math.log(0.4) - 2.3025851 * jax.random.uniform(keys[2], (CHANS, INPUTS), jnp.float32) ** block_scale(keys[2], (CHANS, INPUTS), ((0, 32),), -0.2, 0.2)), 0.04, 0.4)
    model_phase = jnp.clip(jax.random.uniform(keys[3], (CHANS, INPUTS), jnp.float32, -3.140625, 3.140625), -3.140625, 3.140625)
    return dict(voltages=voltages, flags=flags, model_amp=model_amp, model_phase=model_phase)


def window_table():
    index = jnp.arange(TAPS * FRAME, dtype=jnp.float32)
    offset = (index - TAPS * FRAME / 2 + 0.5) / FRAME
    taper = 0.5 - 0.5 * jnp.cos(2.0 * math.pi * (index + 0.5) / (TAPS * FRAME))
    return (jnp.sinc(offset) * taper).reshape(TAPS, FRAME)

def transform_table():
    sample = jnp.arange(FRAME, dtype=jnp.int32)
    channel = BAND_START + jnp.arange(CHANS, dtype=jnp.int32)
    angle = (sample[:, None] * channel[None, :] % FRAME).astype(jnp.float32) * (2.0 * math.pi / FRAME)
    return jnp.stack([jnp.cos(angle), -jnp.sin(angle)], axis=1).astype(jnp.bfloat16)

def channelize(voltages, keep, window, table):
    count = voltages.shape[0]
    samples = voltages.astype(jnp.float32).reshape(count, SPECTRA + TAPS - 1, FRAME)
    frames = window[0] * samples[:, 0:SPECTRA, :]
    for tap in range(1, TAPS):
        frames = frames + window[tap] * samples[:, tap:tap + SPECTRA, :]
    frames = frames.astype(jnp.bfloat16)
    spectra = jnp.einsum('itj,jrc->cirt', frames.astype(jnp.float32), table.astype(jnp.float32), precision=lax.Precision.HIGHEST)
    scale = 1.0 / (64.0 * math.sqrt(FRAME))
    return (spectra * (scale * keep)[None, :, None, None]).astype(jnp.bfloat16)

def sweep(real_part, imag_part, model_re, model_im, gain_re, gain_im):
    probe_re = gain_re * model_re - gain_im * model_im
    probe_im = gain_re * model_im + gain_im * model_re
    power = jnp.sum(probe_re * probe_re + probe_im * probe_im)
    high = lax.Precision.HIGHEST
    product_re = jnp.dot(real_part, probe_re, precision=high) - jnp.dot(imag_part, probe_im, precision=high)
    product_im = jnp.dot(real_part, probe_im, precision=high) + jnp.dot(imag_part, probe_re, precision=high)
    denominator = (model_re * model_re + model_im * model_im) * (power + 1e-06)
    new_re = (model_re * product_re + model_im * product_im) / denominator
    new_im = (model_re * product_im - model_im * product_re) / denominator
    return (new_re, new_im)

def reference(voltages, flags, model_amp, model_phase):
    window = window_table()
    table = transform_table()
    keep = (1 - flags).astype(jnp.float32)
    groups = 16
    per_group = INPUTS // groups
    pieces = lax.map(lambda item: channelize(item[0], item[1], window, table), (voltages.reshape(groups, per_group, SAMPLES), keep.reshape(groups, per_group)))
    spectra = jnp.moveaxis(pieces, 0, 1).reshape(CHANS, INPUTS, 2 * SPECTRA)
    model_re = model_amp * jnp.cos(model_phase)
    model_im = model_amp * jnp.sin(model_phase)

    def one_channel(item):
        rows, chan_re, chan_im = item
        data = rows.astype(jnp.float32)
        turned = jnp.concatenate([data[:, SPECTRA:], -data[:, :SPECTRA]], axis=1)
        real_part = jnp.dot(data, data.T, precision=lax.Precision.HIGHEST, preferred_element_type=jnp.float32) / SPECTRA
        imag_part = jnp.dot(turned, data.T, precision=lax.Precision.HIGHEST, preferred_element_type=jnp.float32) / SPECTRA
        gain_re = jnp.ones((INPUTS,), jnp.float32)
        gain_im = jnp.zeros((INPUTS,), jnp.float32)
        for step in range(ITERS):
            new_re, new_im = sweep(real_part, imag_part, chan_re, chan_im, gain_re, gain_im)
            if step % 2 == 1:
                gain_re = 0.5 * (new_re + gain_re)
                gain_im = 0.5 * (new_im + gain_im)
            else:
                gain_re = new_re
                gain_im = new_im
        return (jnp.stack([real_part, imag_part]).astype(jnp.bfloat16), jnp.stack([gain_re, gain_im]))
    visibility, gains = lax.map(one_channel, (spectra, model_re, model_im))
    return (jnp.moveaxis(visibility, 0, 1), jnp.moveaxis(gains, 0, 1))
```

```python
import math

import jax
import jax.numpy as jnp
from jax import lax
from jax.sharding import PartitionSpec as P

CHANS = 128
FRAME = 512
TAPS = 8
BAND_START = 64
SPECTRA = 256
ITERS = 10


def window_table():
    index = jnp.arange(TAPS * FRAME, dtype=jnp.float32)
    offset = (index - TAPS * FRAME / 2 + 0.5) / FRAME
    taper = 0.5 - 0.5 * jnp.cos(2.0 * math.pi * (index + 0.5) / (TAPS * FRAME))
    return (jnp.sinc(offset) * taper).reshape(TAPS, FRAME)


def transform_table():
    sample = jnp.arange(FRAME, dtype=jnp.int32)
    channel = BAND_START + jnp.arange(CHANS, dtype=jnp.int32)
    angle = (sample[:, None] * channel[None, :] % FRAME).astype(jnp.float32) * (
        2.0 * math.pi / FRAME
    )
    return jnp.stack([jnp.cos(angle), -jnp.sin(angle)], axis=1).astype(jnp.bfloat16)


def channelize(voltages, keep):
    window = window_table()
    table = transform_table()
    count = voltages.shape[0]
    samples = voltages.astype(jnp.float32).reshape(count, SPECTRA + TAPS - 1, FRAME)
    frames = window[0] * samples[:, 0:SPECTRA, :]
    for tap in range(1, TAPS):
        frames = frames + window[tap] * samples[:, tap : tap + SPECTRA, :]
    frames = frames.astype(jnp.bfloat16)
    spectra = jnp.einsum("itj,jrc->cirt", frames, table, preferred_element_type=jnp.float32)
    scale = 1.0 / (64.0 * math.sqrt(FRAME))
    return (spectra * (scale * keep)[None, :, None, None]).astype(jnp.bfloat16)


def split3(value):
    high = value.astype(jnp.bfloat16)
    rest = value - high.astype(jnp.float32)
    mid = rest.astype(jnp.bfloat16)
    low = (rest - mid.astype(jnp.float32)).astype(jnp.bfloat16)
    return jnp.concatenate([high, mid, low], axis=-1)


def exact_dot(lhs, rhs_f32, dims):
    cols = rhs_f32.shape[-1]
    parts = lax.dot_general(
        lhs, split3(rhs_f32), (dims, ((), ())), preferred_element_type=jnp.float32
    )
    return parts[:, :cols] + parts[:, cols : 2 * cols] + parts[:, 2 * cols :]


def solve_gains(data, model_re, model_im):
    count = data.shape[0]

    def sweep(gain_re, gain_im):
        probe_re = gain_re * model_re - gain_im * model_im
        probe_im = gain_re * model_im + gain_im * model_re
        power = jnp.sum(probe_re * probe_re + probe_im * probe_im)
        half = exact_dot(data, jnp.stack([probe_re, probe_im], axis=1), ((0,), (0,)))
        u_re = half[:SPECTRA, 0] + half[SPECTRA:, 1]
        u_im = half[:SPECTRA, 1] - half[SPECTRA:, 0]
        mix = jnp.concatenate(
            [jnp.stack([u_re, u_im], axis=1), jnp.stack([-u_im, u_re], axis=1)], axis=0
        )
        product = exact_dot(data, mix, ((1,), (0,))) * (1.0 / SPECTRA)
        product_re = product[:, 0]
        product_im = product[:, 1]
        denominator = (model_re * model_re + model_im * model_im) * (power + 1e-06)
        new_re = (model_re * product_re + model_im * product_im) / denominator
        new_im = (model_re * product_im - model_im * product_re) / denominator
        return new_re, new_im

    def paired(step_index, carried):
        first_re, first_im = sweep(carried[0], carried[1])
        second_re, second_im = sweep(first_re, first_im)
        return (0.5 * (second_re + first_re), 0.5 * (second_im + first_im))

    start_re = jnp.ones((count,), jnp.float32)
    start_im = jnp.zeros((count,), jnp.float32)
    return lax.fori_loop(0, ITERS // 2, paired, (start_re, start_im))


def shards(voltages, flags, model_amp, model_phase):
    keep = (1 - flags).astype(jnp.float32)
    input_count = voltages.shape[0]
    spectra = channelize(voltages, keep)
    blk_count = lax.axis_size("blk")
    chan_count = lax.axis_size("chan")
    block_index = lax.axis_index("blk")
    turned = lax.all_to_all(spectra, "chan", split_axis=0, concat_axis=1, tiled=True)
    local_chans = turned.shape[0]
    grouped = lax.all_gather(turned, "blk", axis=1, tiled=False)
    grouped = grouped.reshape(local_chans, blk_count, chan_count, input_count, 2 * SPECTRA)
    whole = jnp.swapaxes(grouped, 1, 2).reshape(local_chans, -1, 2 * SPECTRA)
    all_inputs = whole.shape[1]
    row_count = all_inputs // blk_count
    rows = lax.dynamic_slice_in_dim(whole, block_index * row_count, row_count, 1)
    rotated = jnp.concatenate([rows[:, :, SPECTRA:], -rows[:, :, :SPECTRA]], axis=2)
    stacked = jnp.stack([rows, rotated])
    correlation = (
        jnp.einsum("rcpk,cqk->rcpq", stacked, whole, preferred_element_type=jnp.float32) / SPECTRA
    )
    visibility = correlation.astype(jnp.bfloat16)

    solve_chans = local_chans // blk_count
    data = lax.dynamic_slice_in_dim(whole, block_index * solve_chans, solve_chans, 0)
    amp = lax.dynamic_slice_in_dim(model_amp, block_index * solve_chans, solve_chans, 0)
    phase = lax.dynamic_slice_in_dim(model_phase, block_index * solve_chans, solve_chans, 0)
    full_re = amp * jnp.cos(phase)
    full_im = amp * jnp.sin(phase)
    solved = jax.vmap(solve_gains)(data, full_re, full_im)
    solved = jnp.stack(solved)
    owners = solved.reshape(2, solve_chans, chan_count * blk_count, input_count)
    owners = jnp.swapaxes(owners, 1, 2)
    gains = lax.all_to_all(owners, ("chan", "blk"), split_axis=1, concat_axis=1, tiled=True)
    gains = gains.reshape(2, -1, input_count)
    return (visibility, gains)


def solution(mesh):
    return jax.shard_map(
        shards,
        mesh=mesh,
        in_specs=(P(("chan", "blk"), None), P(("chan", "blk")), P("chan", None), P("chan", None)),
        out_specs=(P(None, "chan", "blk", None), P(None, None, ("chan", "blk"))),
        check_vma=False,
    )
```

```python
import math

import jax
import jax.numpy as jnp
from jax import lax
from jax.experimental import pallas as pl
from jax.experimental.pallas import tpu as pltpu
from jax.sharding import PartitionSpec as P

CHANS = 128
FRAME = 512
TAPS = 8
BAND_START = 64
SPECTRA = 256
ITERS = 10


def window_table():
    index = jnp.arange(TAPS * FRAME, dtype=jnp.float32)
    offset = (index - TAPS * FRAME / 2 + 0.5) / FRAME
    taper = 0.5 - 0.5 * jnp.cos(2.0 * math.pi * (index + 0.5) / (TAPS * FRAME))
    return (jnp.sinc(offset) * taper).reshape(TAPS, FRAME)


def transform_table():
    sample = jnp.arange(FRAME, dtype=jnp.int32)
    channel = BAND_START + jnp.arange(CHANS, dtype=jnp.int32)
    angle = (sample[:, None] * channel[None, :] % FRAME).astype(jnp.float32) * (
        2.0 * math.pi / FRAME
    )
    return jnp.stack([jnp.cos(angle), -jnp.sin(angle)], axis=1).astype(jnp.bfloat16)


def channelize(voltages, keep):
    window = window_table()
    table = transform_table()
    count = voltages.shape[0]
    samples = voltages.astype(jnp.float32).reshape(count, SPECTRA + TAPS - 1, FRAME)
    frames = window[0] * samples[:, 0:SPECTRA, :]
    for tap in range(1, TAPS):
        frames = frames + window[tap] * samples[:, tap : tap + SPECTRA, :]
    frames = frames.astype(jnp.bfloat16)
    spectra = jnp.einsum("itj,jrc->cirt", frames, table, preferred_element_type=jnp.float32)
    scale = 1.0 / (64.0 * math.sqrt(FRAME))
    return (spectra * (scale * keep)[None, :, None, None]).astype(jnp.bfloat16)


def split3(value):
    high = value.astype(jnp.bfloat16)
    rest = value - high.astype(jnp.float32)
    mid = rest.astype(jnp.bfloat16)
    low = (rest - mid.astype(jnp.float32)).astype(jnp.bfloat16)
    return jnp.concatenate([high, mid, low], axis=-1)


def exact_dot(lhs, rhs_f32, dims):
    cols = rhs_f32.shape[-1]
    parts = lax.dot_general(
        lhs, split3(rhs_f32), (dims, ((), ())), preferred_element_type=jnp.float32
    )
    return parts[:, :cols] + parts[:, cols : 2 * cols] + parts[:, 2 * cols :]


def solve_gains(data, model_re, model_im):
    count = data.shape[0]

    def sweep(gain_re, gain_im):
        probe_re = gain_re * model_re - gain_im * model_im
        probe_im = gain_re * model_im + gain_im * model_re
        power = jnp.sum(probe_re * probe_re + probe_im * probe_im)
        half = exact_dot(data, jnp.stack([probe_re, probe_im], axis=1), ((0,), (0,)))
        u_re = half[:SPECTRA, 0] + half[SPECTRA:, 1]
        u_im = half[:SPECTRA, 1] - half[SPECTRA:, 0]
        mix = jnp.concatenate(
            [jnp.stack([u_re, u_im], axis=1), jnp.stack([-u_im, u_re], axis=1)], axis=0
        )
        product = exact_dot(data, mix, ((1,), (0,))) * (1.0 / SPECTRA)
        product_re = product[:, 0]
        product_im = product[:, 1]
        denominator = (model_re * model_re + model_im * model_im) * (power + 1e-06)
        new_re = (model_re * product_re + model_im * product_im) / denominator
        new_im = (model_re * product_im - model_im * product_re) / denominator
        return new_re, new_im

    def paired(step_index, carried):
        first_re, first_im = sweep(carried[0], carried[1])
        second_re, second_im = sweep(first_re, first_im)
        return (0.5 * (second_re + first_re), 0.5 * (second_im + first_im))

    start_re = jnp.ones((count,), jnp.float32)
    start_im = jnp.zeros((count,), jnp.float32)
    return lax.fori_loop(0, ITERS // 2, paired, (start_re, start_im))


def correlate_kernel(block_ref, rows_ref, cols_ref, out_ref):
    dims = (((1,), (1,)), ((), ()))
    rows_re = rows_ref[0, :, :SPECTRA]
    rows_im = rows_ref[0, :, SPECTRA:]
    cols_re = cols_ref[0, :, :SPECTRA]
    cols_im = cols_ref[0, :, SPECTRA:]

    def dot(a, b):
        return lax.dot_general(a, b, dims, preferred_element_type=jnp.float32)

    real = dot(rows_re, cols_re) + dot(rows_im, cols_im)
    imag = dot(rows_im, cols_re) - dot(rows_re, cols_im)
    out_ref[0, 0] = (real * (1.0 / SPECTRA)).astype(out_ref.dtype)
    out_ref[1, 0] = (imag * (1.0 / SPECTRA)).astype(out_ref.dtype)


def correlate(whole, block_index, row_count, col_block=512):
    chans, inputs, width = whole.shape
    grid = (chans, inputs // col_block)
    spec = pltpu.PrefetchScalarGridSpec(
        num_scalar_prefetch=1,
        grid=grid,
        in_specs=[
            pl.BlockSpec((1, row_count, width), lambda c, j, blk: (c, blk[0], 0)),
            pl.BlockSpec((1, col_block, width), lambda c, j, blk: (c, j, 0)),
        ],
        out_specs=pl.BlockSpec((2, 1, row_count, col_block), lambda c, j, blk: (0, c, 0, j)),
    )
    flops = 8 * chans * row_count * inputs * (width // 2)
    return pl.pallas_call(
        correlate_kernel,
        grid_spec=spec,
        out_shape=jax.ShapeDtypeStruct((2, chans, row_count, inputs), jnp.bfloat16),
        cost_estimate=pl.CostEstimate(
            flops=flops,
            transcendentals=0,
            bytes_accessed=2 * chans * (inputs * width + row_count * width + 2 * row_count * inputs),
        ),
    )(jnp.reshape(block_index, (1,)).astype(jnp.int32), whole, whole)


def shards(voltages, flags, model_amp, model_phase):
    keep = (1 - flags).astype(jnp.float32)
    input_count = voltages.shape[0]
    spectra = channelize(voltages, keep)
    blk_count = lax.axis_size("blk")
    chan_count = lax.axis_size("chan")
    block_index = lax.axis_index("blk")
    spectra = spectra.reshape(spectra.shape[0], input_count, 2 * SPECTRA)
    turned = lax.all_to_all(spectra, "chan", split_axis=0, concat_axis=1, tiled=True)
    local_chans = turned.shape[0]
    grouped = lax.all_gather(turned, "blk", axis=1, tiled=False)
    grouped = grouped.reshape(local_chans, blk_count, chan_count, input_count, 2 * SPECTRA)
    whole = jnp.swapaxes(grouped, 1, 2).reshape(local_chans, -1, 2 * SPECTRA)
    all_inputs = whole.shape[1]
    row_count = all_inputs // blk_count
    visibility = correlate(whole, block_index, row_count)

    solve_chans = local_chans // blk_count
    data = lax.dynamic_slice_in_dim(whole, block_index * solve_chans, solve_chans, 0)
    amp = lax.dynamic_slice_in_dim(model_amp, block_index * solve_chans, solve_chans, 0)
    phase = lax.dynamic_slice_in_dim(model_phase, block_index * solve_chans, solve_chans, 0)
    full_re = amp * jnp.cos(phase)
    full_im = amp * jnp.sin(phase)
    solved = jax.vmap(solve_gains)(data, full_re, full_im)
    solved = jnp.stack(solved)
    owners = solved.reshape(2, solve_chans, chan_count * blk_count, input_count)
    owners = jnp.swapaxes(owners, 1, 2)
    gains = lax.all_to_all(owners, ("chan", "blk"), split_axis=1, concat_axis=1, tiled=True)
    gains = gains.reshape(2, -1, input_count)
    return (visibility, gains)


def solution(mesh):
    return jax.shard_map(
        shards,
        mesh=mesh,
        in_specs=(P(("chan", "blk"), None), P(("chan", "blk")), P("chan", None), P("chan", None)),
        out_specs=(P(None, "chan", "blk", None), P(None, None, ("chan", "blk"))),
        check_vma=False,
    )
```

```python
import math

import jax
import jax.numpy as jnp
from jax import lax
from jax.experimental import pallas as pl
from jax.experimental.pallas import tpu as pltpu
from jax.sharding import PartitionSpec as P

CHANS = 128
FRAME = 512
TAPS = 8
BAND_START = 64
SPECTRA = 256
ITERS = 10


def window_table():
    index = jnp.arange(TAPS * FRAME, dtype=jnp.float32)
    offset = (index - TAPS * FRAME / 2 + 0.5) / FRAME
    taper = 0.5 - 0.5 * jnp.cos(2.0 * math.pi * (index + 0.5) / (TAPS * FRAME))
    return (jnp.sinc(offset) * taper).reshape(TAPS, FRAME)


def transform_table():
    sample = jnp.arange(FRAME, dtype=jnp.int32)
    channel = BAND_START + jnp.arange(CHANS, dtype=jnp.int32)
    angle = (sample[:, None] * channel[None, :] % FRAME).astype(jnp.float32) * (
        2.0 * math.pi / FRAME
    )
    return jnp.stack([jnp.cos(angle), -jnp.sin(angle)], axis=1).astype(jnp.bfloat16)


def channelize(voltages, keep):
    window = window_table()
    table = transform_table()
    count = voltages.shape[0]
    samples = voltages.astype(jnp.float32).reshape(count, SPECTRA + TAPS - 1, FRAME)
    frames = window[0] * samples[:, 0:SPECTRA, :]
    for tap in range(1, TAPS):
        frames = frames + window[tap] * samples[:, tap : tap + SPECTRA, :]
    frames = frames.astype(jnp.bfloat16)
    spectra = jnp.einsum("itj,jrc->cirt", frames, table, preferred_element_type=jnp.float32)
    scale = 1.0 / (64.0 * math.sqrt(FRAME))
    return (spectra * (scale * keep)[None, :, None, None]).astype(jnp.bfloat16)


def split3(value):
    high = value.astype(jnp.bfloat16)
    rest = value - high.astype(jnp.float32)
    mid = rest.astype(jnp.bfloat16)
    low = (rest - mid.astype(jnp.float32)).astype(jnp.bfloat16)
    return jnp.concatenate([high, mid, low], axis=-1)


def exact_dot(lhs, rhs_f32, dims):
    cols = rhs_f32.shape[-1]
    parts = lax.dot_general(
        lhs, split3(rhs_f32), (dims, ((), ())), preferred_element_type=jnp.float32
    )
    return parts[:, :cols] + parts[:, cols : 2 * cols] + parts[:, 2 * cols :]


def solve_gains(data, model_re, model_im):
    count = data.shape[0]

    def sweep(gain_re, gain_im):
        probe_re = gain_re * model_re - gain_im * model_im
        probe_im = gain_re * model_im + gain_im * model_re
        power = jnp.sum(probe_re * probe_re + probe_im * probe_im)
        half = exact_dot(data, jnp.stack([probe_re, probe_im], axis=1), ((0,), (0,)))
        u_re = half[:SPECTRA, 0] + half[SPECTRA:, 1]
        u_im = half[:SPECTRA, 1] - half[SPECTRA:, 0]
        mix = jnp.concatenate(
            [jnp.stack([u_re, u_im], axis=1), jnp.stack([-u_im, u_re], axis=1)], axis=0
        )
        product = exact_dot(data, mix, ((1,), (0,))) * (1.0 / SPECTRA)
        product_re = product[:, 0]
        product_im = product[:, 1]
        denominator = (model_re * model_re + model_im * model_im) * (power + 1e-06)
        new_re = (model_re * product_re + model_im * product_im) / denominator
        new_im = (model_re * product_im - model_im * product_re) / denominator
        return new_re, new_im

    def paired(step_index, carried):
        first_re, first_im = sweep(carried[0], carried[1])
        second_re, second_im = sweep(first_re, first_im)
        return (0.5 * (second_re + first_re), 0.5 * (second_im + first_im))

    start_re = jnp.ones((count,), jnp.float32)
    start_im = jnp.zeros((count,), jnp.float32)
    return lax.fori_loop(0, ITERS // 2, paired, (start_re, start_im))


def correlate_kernel(block_ref, rows_ref, cols_ref, out_ref):
    dims = (((1,), (1,)), ((), ()))
    rows_re = rows_ref[0, :, :SPECTRA]
    rows_im = rows_ref[0, :, SPECTRA:]
    cols_re = cols_ref[0, :, :SPECTRA]
    cols_im = cols_ref[0, :, SPECTRA:]

    def dot(a, b):
        return lax.dot_general(a, b, dims, preferred_element_type=jnp.float32)

    real = dot(rows_re, cols_re) + dot(rows_im, cols_im)
    imag = dot(rows_im, cols_re) - dot(rows_re, cols_im)
    out_ref[0, 0] = (real * (1.0 / SPECTRA)).astype(out_ref.dtype)
    out_ref[1, 0] = (imag * (1.0 / SPECTRA)).astype(out_ref.dtype)


def correlate(data, scalars, row_count, out=None, total_chans=None, col_block=512):
    chans, inputs, width = data.shape
    total_chans = chans if total_chans is None else total_chans
    grid = (chans, inputs // col_block)
    in_specs = [
        pl.BlockSpec((1, row_count, width), lambda c, j, s: (c, s[0], 0)),
        pl.BlockSpec((1, col_block, width), lambda c, j, s: (c, j, 0)),
    ]
    operands = [scalars, data, data]
    aliases = {}
    if out is not None:
        in_specs.append(pl.BlockSpec(memory_space=pl.ANY))
        operands.append(out)
        aliases = {3: 0}
    spec = pltpu.PrefetchScalarGridSpec(
        num_scalar_prefetch=1,
        grid=grid,
        in_specs=in_specs,
        out_specs=pl.BlockSpec((2, 1, row_count, col_block), lambda c, j, s: (0, s[1] + c, 0, j)),
    )
    flops = 8 * chans * row_count * inputs * (width // 2)
    kernel = correlate_kernel if out is None else correlate_into_kernel
    return pl.pallas_call(
        kernel,
        grid_spec=spec,
        out_shape=jax.ShapeDtypeStruct((2, total_chans, row_count, inputs), jnp.bfloat16),
        input_output_aliases=aliases,
        cost_estimate=pl.CostEstimate(
            flops=flops,
            transcendentals=0,
            bytes_accessed=2 * chans * (inputs * width + row_count * width + 2 * row_count * inputs),
        ),
    )(*operands)


def correlate_into_kernel(block_ref, rows_ref, cols_ref, prev_ref, out_ref):
    correlate_kernel(block_ref, rows_ref, cols_ref, out_ref)


def shards(voltages, flags, model_amp, model_phase):
    keep = (1 - flags).astype(jnp.float32)
    input_count = voltages.shape[0]
    spectra = channelize(voltages, keep)
    blk_count = lax.axis_size("blk")
    chan_count = lax.axis_size("chan")
    block_index = lax.axis_index("blk")
    spectra = spectra.reshape(chan_count, 2, 2, input_count, 2 * SPECTRA)
    send = jnp.broadcast_to(
        spectra[:, None], (chan_count, 2, 2, 2, input_count, 2 * SPECTRA)
    )
    send = send.reshape(chan_count * blk_count, 2, input_count, 2 * SPECTRA)
    send = jnp.swapaxes(send, 0, 1)
    got = lax.all_to_all(send, ("chan", "blk"), split_axis=1, concat_axis=1, tiled=True)
    mine = got.reshape(2, -1, 2 * SPECTRA)
    all_inputs = mine.shape[1]
    row_count = all_inputs // blk_count
    core = block_index % 2
    level = block_index // 2
    theirs = lax.ppermute(mine, "blk", perm=[(b, b ^ 1) for b in range(blk_count)])
    local_chans = 4
    first = jnp.stack([block_index, 2 * core]).astype(jnp.int32)
    second = jnp.stack([block_index, 2 - 2 * core]).astype(jnp.int32)
    visibility = correlate(mine, first, row_count, total_chans=local_chans)
    visibility = correlate(theirs, second, row_count, out=visibility, total_chans=local_chans)

    data = lax.dynamic_index_in_dim(mine, level, 0, keepdims=False)
    solve = 2 * core + level
    amp = lax.dynamic_index_in_dim(model_amp, solve, 0, keepdims=False)
    phase = lax.dynamic_index_in_dim(model_phase, solve, 0, keepdims=False)
    full_re = amp * jnp.cos(phase)
    full_im = amp * jnp.sin(phase)
    solved = jnp.stack(solve_gains(data, full_re, full_im))
    owners = solved.reshape(2, chan_count * blk_count, 1, input_count)
    gains = lax.all_to_all(owners, ("chan", "blk"), split_axis=1, concat_axis=1, tiled=True)
    gains = gains.reshape(2, chan_count, 2, 2, input_count)
    gains = jnp.swapaxes(gains, 2, 3).reshape(2, -1, input_count)
    return (visibility, gains)


def solution(mesh):
    return jax.shard_map(
        shards,
        mesh=mesh,
        in_specs=(P(("chan", "blk"), None), P(("chan", "blk")), P("chan", None), P("chan", None)),
        out_specs=(P(None, "chan", "blk", None), P(None, None, ("chan", "blk"))),
        check_vma=False,
    )
```

```python
import math

import jax
import jax.numpy as jnp
from jax import lax
from jax.experimental import pallas as pl
from jax.experimental.pallas import tpu as pltpu
from jax.sharding import PartitionSpec as P

CHANS = 128
FRAME = 512
TAPS = 8
BAND_START = 64
SPECTRA = 256
ITERS = 10


def window_table():
    index = jnp.arange(TAPS * FRAME, dtype=jnp.float32)
    offset = (index - TAPS * FRAME / 2 + 0.5) / FRAME
    taper = 0.5 - 0.5 * jnp.cos(2.0 * math.pi * (index + 0.5) / (TAPS * FRAME))
    return (jnp.sinc(offset) * taper).reshape(TAPS, FRAME)


def transform_table():
    sample = jnp.arange(FRAME, dtype=jnp.int32)
    channel = BAND_START + jnp.arange(CHANS, dtype=jnp.int32)
    angle = (sample[:, None] * channel[None, :] % FRAME).astype(jnp.float32) * (
        2.0 * math.pi / FRAME
    )
    return jnp.stack([jnp.cos(angle), -jnp.sin(angle)], axis=1).astype(jnp.bfloat16)


def transform_kernel(keep_ref, table_ref, frames_ref, out_ref):
    group = frames_ref.shape[0]
    base = pl.program_id(0) * group
    scale = 1.0 / (64.0 * math.sqrt(FRAME))
    for item in range(group):
        result = lax.dot_general(
            table_ref[...], frames_ref[item], (((1,), (1,)), ((), ())),
            preferred_element_type=jnp.float32,
        )
        result = result * (scale * keep_ref[base + item])
        out_ref[:, item, :SPECTRA] = result[:CHANS].astype(out_ref.dtype)
        out_ref[:, item, SPECTRA:] = result[CHANS:].astype(out_ref.dtype)


def channelize(voltages, keep):
    window = window_table()
    table = transform_table()
    count = voltages.shape[0]
    samples = voltages.astype(jnp.bfloat16).reshape(count, SPECTRA + TAPS - 1, FRAME)
    frames = window[0] * samples[:, 0:SPECTRA, :].astype(jnp.float32)
    for tap in range(1, TAPS):
        frames = frames + window[tap] * samples[:, tap : tap + SPECTRA, :].astype(jnp.float32)
    frames = frames.astype(jnp.bfloat16)
    table_t = jnp.transpose(table.reshape(FRAME, 2 * CHANS))
    group = 8
    return pl.pallas_call(
        transform_kernel,
        grid=(count // group,),
        in_specs=[
            pl.BlockSpec(memory_space=pltpu.SMEM),
            pl.BlockSpec((2 * CHANS, FRAME), lambda g: (0, 0)),
            pl.BlockSpec((group, SPECTRA, FRAME), lambda g: (g, 0, 0)),
        ],
        out_specs=pl.BlockSpec((CHANS, group, 2 * SPECTRA), lambda g: (0, g, 0)),
        out_shape=jax.ShapeDtypeStruct((CHANS, count, 2 * SPECTRA), jnp.bfloat16),
        cost_estimate=pl.CostEstimate(
            flops=2 * count * SPECTRA * FRAME * 2 * CHANS,
            transcendentals=0,
            bytes_accessed=2 * count * SPECTRA * FRAME + 2 * CHANS * count * 2 * SPECTRA,
        ),
    )(keep, table_t, frames)


def split3(value):
    high = value.astype(jnp.bfloat16)
    rest = value - high.astype(jnp.float32)
    mid = rest.astype(jnp.bfloat16)
    low = (rest - mid.astype(jnp.float32)).astype(jnp.bfloat16)
    return jnp.concatenate([high, mid, low], axis=-1)


def exact_dot(lhs, rhs_f32, dims):
    cols = rhs_f32.shape[-1]
    parts = lax.dot_general(
        lhs, split3(rhs_f32), (dims, ((), ())), preferred_element_type=jnp.float32
    )
    return parts[:, :cols] + parts[:, cols : 2 * cols] + parts[:, 2 * cols :]


def solve_gains(data, model_re, model_im):
    count = data.shape[0]

    def sweep(gain_re, gain_im):
        probe_re = gain_re * model_re - gain_im * model_im
        probe_im = gain_re * model_im + gain_im * model_re
        power = jnp.sum(probe_re * probe_re + probe_im * probe_im)
        half = exact_dot(data, jnp.stack([probe_re, probe_im], axis=1), ((0,), (0,)))
        u_re = half[:SPECTRA, 0] + half[SPECTRA:, 1]
        u_im = half[:SPECTRA, 1] - half[SPECTRA:, 0]
        mix = jnp.concatenate(
            [jnp.stack([u_re, u_im], axis=1), jnp.stack([-u_im, u_re], axis=1)], axis=0
        )
        product = exact_dot(data, mix, ((1,), (0,))) * (1.0 / SPECTRA)
        product_re = product[:, 0]
        product_im = product[:, 1]
        denominator = (model_re * model_re + model_im * model_im) * (power + 1e-06)
        new_re = (model_re * product_re + model_im * product_im) / denominator
        new_im = (model_re * product_im - model_im * product_re) / denominator
        return new_re, new_im

    def paired(step_index, carried):
        first_re, first_im = sweep(carried[0], carried[1])
        second_re, second_im = sweep(first_re, first_im)
        return (0.5 * (second_re + first_re), 0.5 * (second_im + first_im))

    start_re = jnp.ones((count,), jnp.float32)
    start_im = jnp.zeros((count,), jnp.float32)
    return lax.fori_loop(0, ITERS // 2, paired, (start_re, start_im))


def correlate_kernel(block_ref, rows_ref, cols_ref, out_ref):
    dims = (((1,), (1,)), ((), ()))
    rows_re = rows_ref[0, :, :SPECTRA]
    rows_im = rows_ref[0, :, SPECTRA:]
    cols_re = cols_ref[0, :, :SPECTRA]
    cols_im = cols_ref[0, :, SPECTRA:]

    def dot(a, b):
        return lax.dot_general(a, b, dims, preferred_element_type=jnp.float32)

    real = dot(rows_re, cols_re) + dot(rows_im, cols_im)
    imag = dot(rows_im, cols_re) - dot(rows_re, cols_im)
    out_ref[0, 0] = (real * (1.0 / SPECTRA)).astype(out_ref.dtype)
    out_ref[1, 0] = (imag * (1.0 / SPECTRA)).astype(out_ref.dtype)


def correlate(data, scalars, row_count, out=None, total_chans=None, col_block=512):
    chans, inputs, width = data.shape
    total_chans = chans if total_chans is None else total_chans
    grid = (chans, inputs // col_block)
    in_specs = [
        pl.BlockSpec((1, row_count, width), lambda c, j, s: (c, s[0], 0)),
        pl.BlockSpec((1, col_block, width), lambda c, j, s: (c, j, 0)),
    ]
    operands = [scalars, data, data]
    aliases = {}
    if out is not None:
        in_specs.append(pl.BlockSpec(memory_space=pl.ANY))
        operands.append(out)
        aliases = {3: 0}
    spec = pltpu.PrefetchScalarGridSpec(
        num_scalar_prefetch=1,
        grid=grid,
        in_specs=in_specs,
        out_specs=pl.BlockSpec((2, 1, row_count, col_block), lambda c, j, s: (0, s[1] + c, 0, j)),
    )
    flops = 8 * chans * row_count * inputs * (width // 2)
    kernel = correlate_kernel if out is None else correlate_into_kernel
    return pl.pallas_call(
        kernel,
        grid_spec=spec,
        out_shape=jax.ShapeDtypeStruct((2, total_chans, row_count, inputs), jnp.bfloat16),
        input_output_aliases=aliases,
        cost_estimate=pl.CostEstimate(
            flops=flops,
            transcendentals=0,
            bytes_accessed=2 * chans * (inputs * width + row_count * width + 2 * row_count * inputs),
        ),
    )(*operands)


def correlate_into_kernel(block_ref, rows_ref, cols_ref, prev_ref, out_ref):
    correlate_kernel(block_ref, rows_ref, cols_ref, out_ref)


def shards(voltages, flags, model_amp, model_phase):
    keep = (1 - flags).astype(jnp.float32)
    input_count = voltages.shape[0]
    spectra = channelize(voltages, keep)
    blk_count = lax.axis_size("blk")
    chan_count = lax.axis_size("chan")
    block_index = lax.axis_index("blk")
    spectra = spectra.reshape(chan_count, 2, 2, input_count, 2 * SPECTRA)
    send = jnp.broadcast_to(
        spectra[:, None], (chan_count, 2, 2, 2, input_count, 2 * SPECTRA)
    )
    send = send.reshape(chan_count * blk_count, 2, input_count, 2 * SPECTRA)
    send = jnp.swapaxes(send, 0, 1)
    got = lax.all_to_all(send, ("chan", "blk"), split_axis=1, concat_axis=1, tiled=True)
    mine = got.reshape(2, -1, 2 * SPECTRA)
    all_inputs = mine.shape[1]
    row_count = all_inputs // blk_count
    core = block_index % 2
    level = block_index // 2
    theirs = lax.ppermute(mine, "blk", perm=[(b, b ^ 1) for b in range(blk_count)])
    local_chans = 4
    first = jnp.stack([block_index, 2 * core]).astype(jnp.int32)
    second = jnp.stack([block_index, 2 - 2 * core]).astype(jnp.int32)
    visibility = correlate(mine, first, row_count, total_chans=local_chans)
    visibility = correlate(theirs, second, row_count, out=visibility, total_chans=local_chans)

    data = lax.dynamic_index_in_dim(mine, level, 0, keepdims=False)
    solve = 2 * core + level
    amp = lax.dynamic_index_in_dim(model_amp, solve, 0, keepdims=False)
    phase = lax.dynamic_index_in_dim(model_phase, solve, 0, keepdims=False)
    full_re = amp * jnp.cos(phase)
    full_im = amp * jnp.sin(phase)
    solved = jnp.stack(solve_gains(data, full_re, full_im))
    owners = solved.reshape(2, chan_count * blk_count, 1, input_count)
    gains = lax.all_to_all(owners, ("chan", "blk"), split_axis=1, concat_axis=1, tiled=True)
    gains = gains.reshape(2, chan_count, 2, 2, input_count)
    gains = jnp.swapaxes(gains, 2, 3).reshape(2, -1, input_count)
    return (visibility, gains)


def solution(mesh):
    return jax.shard_map(
        shards,
        mesh=mesh,
        in_specs=(P(("chan", "blk"), None), P(("chan", "blk")), P("chan", None), P("chan", None)),
        out_specs=(P(None, "chan", "blk", None), P(None, None, ("chan", "blk"))),
        check_vma=False,
    )
```

```python
import math

import jax
import jax.numpy as jnp
from jax import lax
from jax.experimental import pallas as pl
from jax.experimental.pallas import tpu as pltpu
from jax.sharding import PartitionSpec as P

CHANS = 128
FRAME = 512
TAPS = 8
BAND_START = 64
SPECTRA = 256
ITERS = 10


def window_table():
    index = jnp.arange(TAPS * FRAME, dtype=jnp.float32)
    offset = (index - TAPS * FRAME / 2 + 0.5) / FRAME
    taper = 0.5 - 0.5 * jnp.cos(2.0 * math.pi * (index + 0.5) / (TAPS * FRAME))
    return (jnp.sinc(offset) * taper).reshape(TAPS, FRAME)


def transform_table():
    sample = jnp.arange(FRAME, dtype=jnp.int32)
    channel = BAND_START + jnp.arange(CHANS, dtype=jnp.int32)
    angle = (sample[:, None] * channel[None, :] % FRAME).astype(jnp.float32) * (
        2.0 * math.pi / FRAME
    )
    return jnp.stack([jnp.cos(angle), -jnp.sin(angle)], axis=1).astype(jnp.bfloat16)


def transform_kernel(frames_ref, table_ref, keep_ref, out_ref):
    count, width = frames_ref.shape
    steps = width // FRAME
    stacked = jnp.concatenate(
        [frames_ref[:, step * FRAME : (step + 1) * FRAME] for step in range(steps)], axis=0
    )
    result = jnp.dot(stacked, table_ref[...], preferred_element_type=jnp.float32)
    result = result * keep_ref[...]
    out_ref[...] = result.astype(out_ref.dtype).reshape(out_ref.shape)


def channelize(voltages, keep):
    window = window_table()
    table = transform_table()
    count = voltages.shape[0]
    span = SPECTRA * FRAME
    def weight(tap):
        return jnp.broadcast_to(window[tap][None, None, :], (count, SPECTRA, FRAME)).reshape(
            count, span
        )

    frames = weight(0) * voltages[:, 0:span].astype(jnp.float32)
    for tap in range(1, TAPS):
        frames = frames + weight(tap) * voltages[:, tap * FRAME : tap * FRAME + span].astype(
            jnp.float32
        )
    frames = frames.astype(jnp.bfloat16)
    table = table.reshape(FRAME, 2 * CHANS)
    scale = 1.0 / (64.0 * math.sqrt(FRAME))
    chunk = 32
    keep_rows = jnp.tile(scale * keep, chunk)[:, None]
    return pl.pallas_call(
        transform_kernel,
        grid=(SPECTRA // chunk,),
        in_specs=[
            pl.BlockSpec((count, chunk * FRAME), lambda g: (0, g)),
            pl.BlockSpec((FRAME, 2 * CHANS), lambda g: (0, 0)),
            pl.BlockSpec((chunk * count, 1), lambda g: (0, 0)),
        ],
        out_specs=pl.BlockSpec((chunk, count, 2 * CHANS), lambda g: (g, 0, 0)),
        out_shape=jax.ShapeDtypeStruct((SPECTRA, count, 2 * CHANS), jnp.bfloat16),
        cost_estimate=pl.CostEstimate(
            flops=2 * count * SPECTRA * FRAME * 2 * CHANS,
            transcendentals=0,
            bytes_accessed=2 * count * SPECTRA * FRAME + 2 * CHANS * count * 2 * SPECTRA,
        ),
    )(frames, table, keep_rows)


def split3(value):
    high = value.astype(jnp.bfloat16)
    rest = value - high.astype(jnp.float32)
    mid = rest.astype(jnp.bfloat16)
    low = (rest - mid.astype(jnp.float32)).astype(jnp.bfloat16)
    return jnp.concatenate([high, mid, low], axis=-1)


def exact_dot(lhs, rhs_f32, dims):
    cols = rhs_f32.shape[-1]
    parts = lax.dot_general(
        lhs, split3(rhs_f32), (dims, ((), ())), preferred_element_type=jnp.float32
    )
    return parts[:, :cols] + parts[:, cols : 2 * cols] + parts[:, 2 * cols :]


def solve_gains(data, model_re, model_im):
    count = data.shape[0]

    def sweep(gain_re, gain_im):
        probe_re = gain_re * model_re - gain_im * model_im
        probe_im = gain_re * model_im + gain_im * model_re
        power = jnp.sum(probe_re * probe_re + probe_im * probe_im)
        half = exact_dot(data, jnp.stack([probe_re, probe_im], axis=1), ((0,), (0,)))
        u_re = half[:SPECTRA, 0] + half[SPECTRA:, 1]
        u_im = half[:SPECTRA, 1] - half[SPECTRA:, 0]
        mix = jnp.concatenate(
            [jnp.stack([u_re, u_im], axis=1), jnp.stack([-u_im, u_re], axis=1)], axis=0
        )
        product = exact_dot(data, mix, ((1,), (0,))) * (1.0 / SPECTRA)
        product_re = product[:, 0]
        product_im = product[:, 1]
        denominator = (model_re * model_re + model_im * model_im) * (power + 1e-06)
        new_re = (model_re * product_re + model_im * product_im) / denominator
        new_im = (model_re * product_im - model_im * product_re) / denominator
        return new_re, new_im

    def paired(step_index, carried):
        first_re, first_im = sweep(carried[0], carried[1])
        second_re, second_im = sweep(first_re, first_im)
        return (0.5 * (second_re + first_re), 0.5 * (second_im + first_im))

    start_re = jnp.ones((count,), jnp.float32)
    start_im = jnp.zeros((count,), jnp.float32)
    return lax.fori_loop(0, ITERS // 2, paired, (start_re, start_im))


def correlate_kernel(block_ref, rows_ref, cols_ref, out_ref):
    dims = (((1,), (1,)), ((), ()))
    rows_re = rows_ref[0, :, :SPECTRA]
    rows_im = rows_ref[0, :, SPECTRA:]
    cols_re = cols_ref[0, :, :SPECTRA]
    cols_im = cols_ref[0, :, SPECTRA:]

    def dot(a, b):
        return lax.dot_general(a, b, dims, preferred_element_type=jnp.float32)

    real = dot(rows_re, cols_re) + dot(rows_im, cols_im)
    imag = dot(rows_im, cols_re) - dot(rows_re, cols_im)
    out_ref[0, 0] = (real * (1.0 / SPECTRA)).astype(out_ref.dtype)
    out_ref[1, 0] = (imag * (1.0 / SPECTRA)).astype(out_ref.dtype)


def correlate(data, scalars, row_count, out=None, total_chans=None, col_block=512):
    chans, inputs, width = data.shape
    total_chans = chans if total_chans is None else total_chans
    grid = (chans, inputs // col_block)
    in_specs = [
        pl.BlockSpec((1, row_count, width), lambda c, j, s: (c, s[0], 0)),
        pl.BlockSpec((1, col_block, width), lambda c, j, s: (c, j, 0)),
    ]
    operands = [scalars, data, data]
    aliases = {}
    if out is not None:
        in_specs.append(pl.BlockSpec(memory_space=pl.ANY))
        operands.append(out)
        aliases = {3: 0}
    spec = pltpu.PrefetchScalarGridSpec(
        num_scalar_prefetch=1,
        grid=grid,
        in_specs=in_specs,
        out_specs=pl.BlockSpec((2, 1, row_count, col_block), lambda c, j, s: (0, s[1] + c, 0, j)),
    )
    flops = 8 * chans * row_count * inputs * (width // 2)
    kernel = correlate_kernel if out is None else correlate_into_kernel
    return pl.pallas_call(
        kernel,
        grid_spec=spec,
        out_shape=jax.ShapeDtypeStruct((2, total_chans, row_count, inputs), jnp.bfloat16),
        input_output_aliases=aliases,
        cost_estimate=pl.CostEstimate(
            flops=flops,
            transcendentals=0,
            bytes_accessed=2 * chans * (inputs * width + row_count * width + 2 * row_count * inputs),
        ),
    )(*operands)


def correlate_into_kernel(block_ref, rows_ref, cols_ref, prev_ref, out_ref):
    correlate_kernel(block_ref, rows_ref, cols_ref, out_ref)


def shards(voltages, flags, model_amp, model_phase):
    keep = (1 - flags).astype(jnp.float32)
    input_count = voltages.shape[0]
    spectra = channelize(voltages, keep)
    blk_count = lax.axis_size("blk")
    chan_count = lax.axis_size("chan")
    block_index = lax.axis_index("blk")
    spectra = spectra.reshape(SPECTRA, input_count, 2, chan_count, 2, 2)
    spectra = jnp.transpose(spectra, (5, 3, 4, 1, 2, 0))
    send = jnp.broadcast_to(
        spectra[:, :, None], (2, chan_count, 2, 2, input_count, 2, SPECTRA)
    )
    send = send.reshape(2, chan_count * blk_count, input_count, 2 * SPECTRA)
    got = lax.all_to_all(send, ("chan", "blk"), split_axis=1, concat_axis=1, tiled=True)
    mine = got.reshape(2, -1, 2 * SPECTRA)
    all_inputs = mine.shape[1]
    row_count = all_inputs // blk_count
    core = block_index % 2
    level = block_index // 2
    theirs = lax.ppermute(mine, "blk", perm=[(b, b ^ 1) for b in range(blk_count)])
    local_chans = 4
    first = jnp.stack([block_index, 2 * core]).astype(jnp.int32)
    second = jnp.stack([block_index, 2 - 2 * core]).astype(jnp.int32)
    visibility = correlate(mine, first, row_count, total_chans=local_chans)
    visibility = correlate(theirs, second, row_count, out=visibility, total_chans=local_chans)

    data = lax.dynamic_index_in_dim(mine, level, 0, keepdims=False)
    solve = 2 * core + level
    amp = lax.dynamic_index_in_dim(model_amp, solve, 0, keepdims=False)
    phase = lax.dynamic_index_in_dim(model_phase, solve, 0, keepdims=False)
    full_re = amp * jnp.cos(phase)
    full_im = amp * jnp.sin(phase)
    solved = jnp.stack(solve_gains(data, full_re, full_im))
    owners = solved.reshape(2, chan_count * blk_count, 1, input_count)
    gains = lax.all_to_all(owners, ("chan", "blk"), split_axis=1, concat_axis=1, tiled=True)
    gains = gains.reshape(2, chan_count, 2, 2, input_count)
    gains = jnp.swapaxes(gains, 2, 3).reshape(2, -1, input_count)
    return (visibility, gains)


def solution(mesh):
    return jax.shard_map(
        shards,
        mesh=mesh,
        in_specs=(P(("chan", "blk"), None), P(("chan", "blk")), P("chan", None), P("chan", None)),
        out_specs=(P(None, "chan", "blk", None), P(None, None, ("chan", "blk"))),
        check_vma=False,
    )
```

```python
import math

import jax
import jax.numpy as jnp
from jax import lax
from jax.experimental import pallas as pl
from jax.experimental.pallas import tpu as pltpu
from jax.sharding import PartitionSpec as P

CHANS = 128
FRAME = 512
TAPS = 8
BAND_START = 64
SPECTRA = 256
ITERS = 10


def window_table():
    index = jnp.arange(TAPS * FRAME, dtype=jnp.float32)
    offset = (index - TAPS * FRAME / 2 + 0.5) / FRAME
    taper = 0.5 - 0.5 * jnp.cos(2.0 * math.pi * (index + 0.5) / (TAPS * FRAME))
    return (jnp.sinc(offset) * taper).reshape(TAPS, FRAME)


def transform_table():
    sample = jnp.arange(FRAME, dtype=jnp.int32)
    channel = BAND_START + jnp.arange(CHANS, dtype=jnp.int32)
    angle = (sample[:, None] * channel[None, :] % FRAME).astype(jnp.float32) * (
        2.0 * math.pi / FRAME
    )
    return jnp.stack([jnp.cos(angle), -jnp.sin(angle)], axis=1).astype(jnp.bfloat16)


def transform_kernel(keep_ref, window_ref, table_ref, samples_ref, out_ref, wide_ref):
    group = samples_ref.shape[0]
    base = pl.program_id(0) * group
    scale = 1.0 / (64.0 * math.sqrt(FRAME))
    for item in range(group):
        wide_ref[0 : SPECTRA + TAPS - 1, :] = samples_ref[item].astype(jnp.float32)
        frames = window_ref[0:1, :] * wide_ref[0:SPECTRA, :]
        for tap in range(1, TAPS):
            frames = frames + window_ref[tap : tap + 1, :] * wide_ref[tap : tap + SPECTRA, :]
        result = lax.dot_general(
            table_ref[...], frames.astype(jnp.bfloat16), (((1,), (1,)), ((), ())),
            preferred_element_type=jnp.float32,
        )
        result = result * (scale * keep_ref[base + item])
        out_ref[:, item, :SPECTRA] = result[:CHANS].astype(out_ref.dtype)
        out_ref[:, item, SPECTRA:] = result[CHANS:].astype(out_ref.dtype)


def channelize(voltages, keep):
    window = window_table()
    table = transform_table()
    count = voltages.shape[0]
    samples = voltages.astype(jnp.bfloat16).reshape(count, SPECTRA + TAPS - 1, FRAME)
    table_t = jnp.transpose(table.reshape(FRAME, 2 * CHANS))
    group = 8
    return pl.pallas_call(
        transform_kernel,
        grid=(count // group,),
        in_specs=[
            pl.BlockSpec(memory_space=pltpu.SMEM),
            pl.BlockSpec((TAPS, FRAME), lambda g: (0, 0)),
            pl.BlockSpec((2 * CHANS, FRAME), lambda g: (0, 0)),
            pl.BlockSpec((group, SPECTRA + TAPS - 1, FRAME), lambda g: (g, 0, 0)),
        ],
        out_specs=pl.BlockSpec((CHANS, group, 2 * SPECTRA), lambda g: (0, g, 0)),
        out_shape=jax.ShapeDtypeStruct((CHANS, count, 2 * SPECTRA), jnp.bfloat16),
        scratch_shapes=[pltpu.VMEM((SPECTRA + 2 * TAPS, FRAME), jnp.float32)],
        cost_estimate=pl.CostEstimate(
            flops=2 * count * SPECTRA * FRAME * (2 * CHANS + TAPS),
            transcendentals=0,
            bytes_accessed=2 * count * (SPECTRA + TAPS) * FRAME + 2 * CHANS * count * 2 * SPECTRA,
        ),
    )(keep, window, table_t, samples)


def split3(value):
    high = value.astype(jnp.bfloat16)
    rest = value - high.astype(jnp.float32)
    mid = rest.astype(jnp.bfloat16)
    low = (rest - mid.astype(jnp.float32)).astype(jnp.bfloat16)
    return jnp.concatenate([high, mid, low], axis=-1)


def exact_dot(lhs, rhs_f32, dims):
    cols = rhs_f32.shape[-1]
    parts = lax.dot_general(
        lhs, split3(rhs_f32), (dims, ((), ())), preferred_element_type=jnp.float32
    )
    return parts[:, :cols] + parts[:, cols : 2 * cols] + parts[:, 2 * cols :]


def solve_gains(data, model_re, model_im):
    count = data.shape[0]

    def sweep(gain_re, gain_im):
        probe_re = gain_re * model_re - gain_im * model_im
        probe_im = gain_re * model_im + gain_im * model_re
        power = jnp.sum(probe_re * probe_re + probe_im * probe_im)
        half = exact_dot(data, jnp.stack([probe_re, probe_im], axis=1), ((0,), (0,)))
        u_re = half[:SPECTRA, 0] + half[SPECTRA:, 1]
        u_im = half[:SPECTRA, 1] - half[SPECTRA:, 0]
        mix = jnp.concatenate(
            [jnp.stack([u_re, u_im], axis=1), jnp.stack([-u_im, u_re], axis=1)], axis=0
        )
        product = exact_dot(data, mix, ((1,), (0,))) * (1.0 / SPECTRA)
        product_re = product[:, 0]
        product_im = product[:, 1]
        denominator = (model_re * model_re + model_im * model_im) * (power + 1e-06)
        new_re = (model_re * product_re + model_im * product_im) / denominator
        new_im = (model_re * product_im - model_im * product_re) / denominator
        return new_re, new_im

    def paired(step_index, carried):
        first_re, first_im = sweep(carried[0], carried[1])
        second_re, second_im = sweep(first_re, first_im)
        return (0.5 * (second_re + first_re), 0.5 * (second_im + first_im))

    start_re = jnp.ones((count,), jnp.float32)
    start_im = jnp.zeros((count,), jnp.float32)
    return lax.fori_loop(0, ITERS // 2, paired, (start_re, start_im))


def correlate_kernel(block_ref, rows_ref, cols_ref, out_ref):
    dims = (((1,), (1,)), ((), ()))
    rows_re = rows_ref[0, :, :SPECTRA]
    rows_im = rows_ref[0, :, SPECTRA:]
    cols_re = cols_ref[0, :, :SPECTRA]
    cols_im = cols_ref[0, :, SPECTRA:]

    def dot(a, b):
        return lax.dot_general(a, b, dims, preferred_element_type=jnp.float32)

    real = dot(rows_re, cols_re) + dot(rows_im, cols_im)
    imag = dot(rows_im, cols_re) - dot(rows_re, cols_im)
    out_ref[0, 0] = (real * (1.0 / SPECTRA)).astype(out_ref.dtype)
    out_ref[1, 0] = (imag * (1.0 / SPECTRA)).astype(out_ref.dtype)


def correlate(data, scalars, row_count, out=None, total_chans=None, col_block=512):
    chans, inputs, width = data.shape
    total_chans = chans if total_chans is None else total_chans
    grid = (chans, inputs // col_block)
    in_specs = [
        pl.BlockSpec((1, row_count, width), lambda c, j, s: (c, s[0], 0)),
        pl.BlockSpec((1, col_block, width), lambda c, j, s: (c, j, 0)),
    ]
    operands = [scalars, data, data]
    aliases = {}
    if out is not None:
        in_specs.append(pl.BlockSpec(memory_space=pl.ANY))
        operands.append(out)
        aliases = {3: 0}
    spec = pltpu.PrefetchScalarGridSpec(
        num_scalar_prefetch=1,
        grid=grid,
        in_specs=in_specs,
        out_specs=pl.BlockSpec((2, 1, row_count, col_block), lambda c, j, s: (0, s[1] + c, 0, j)),
    )
    flops = 8 * chans * row_count * inputs * (width // 2)
    kernel = correlate_kernel if out is None else correlate_into_kernel
    return pl.pallas_call(
        kernel,
        grid_spec=spec,
        out_shape=jax.ShapeDtypeStruct((2, total_chans, row_count, inputs), jnp.bfloat16),
        input_output_aliases=aliases,
        cost_estimate=pl.CostEstimate(
            flops=flops,
            transcendentals=0,
            bytes_accessed=2 * chans * (inputs * width + row_count * width + 2 * row_count * inputs),
        ),
    )(*operands)


def correlate_into_kernel(block_ref, rows_ref, cols_ref, prev_ref, out_ref):
    correlate_kernel(block_ref, rows_ref, cols_ref, out_ref)


def shards(voltages, flags, model_amp, model_phase):
    keep = (1 - flags).astype(jnp.float32)
    input_count = voltages.shape[0]
    spectra = channelize(voltages, keep)
    blk_count = lax.axis_size("blk")
    chan_count = lax.axis_size("chan")
    block_index = lax.axis_index("blk")
    spectra = spectra.reshape(chan_count, 2, 2, input_count, 2 * SPECTRA)
    send = jnp.broadcast_to(
        spectra[:, None], (chan_count, 2, 2, 2, input_count, 2 * SPECTRA)
    )
    send = send.reshape(chan_count * blk_count, 2, input_count, 2 * SPECTRA)
    send = jnp.swapaxes(send, 0, 1)
    got = lax.all_to_all(send, ("chan", "blk"), split_axis=1, concat_axis=1, tiled=True)
    mine = got.reshape(2, -1, 2 * SPECTRA)
    all_inputs = mine.shape[1]
    row_count = all_inputs // blk_count
    core = block_index % 2
    level = block_index // 2
    theirs = lax.ppermute(mine, "blk", perm=[(b, b ^ 1) for b in range(blk_count)])
    local_chans = 4
    first = jnp.stack([block_index, 2 * core]).astype(jnp.int32)
    second = jnp.stack([block_index, 2 - 2 * core]).astype(jnp.int32)
    visibility = correlate(mine, first, row_count, total_chans=local_chans)
    visibility = correlate(theirs, second, row_count, out=visibility, total_chans=local_chans)

    data = lax.dynamic_index_in_dim(mine, level, 0, keepdims=False)
    solve = 2 * core + level
    amp = lax.dynamic_index_in_dim(model_amp, solve, 0, keepdims=False)
    phase = lax.dynamic_index_in_dim(model_phase, solve, 0, keepdims=False)
    full_re = amp * jnp.cos(phase)
    full_im = amp * jnp.sin(phase)
    solved = jnp.stack(solve_gains(data, full_re, full_im))
    owners = solved.reshape(2, chan_count * blk_count, 1, input_count)
    gains = lax.all_to_all(owners, ("chan", "blk"), split_axis=1, concat_axis=1, tiled=True)
    gains = gains.reshape(2, chan_count, 2, 2, input_count)
    gains = jnp.swapaxes(gains, 2, 3).reshape(2, -1, input_count)
    return (visibility, gains)


def solution(mesh):
    return jax.shard_map(
        shards,
        mesh=mesh,
        in_specs=(P(("chan", "blk"), None), P(("chan", "blk")), P("chan", None), P("chan", None)),
        out_specs=(P(None, "chan", "blk", None), P(None, None, ("chan", "blk"))),
        check_vma=False,
    )
```

```python
import math

import jax
import jax.numpy as jnp
from jax import lax
from jax.experimental import pallas as pl
from jax.experimental.pallas import tpu as pltpu
from jax.sharding import PartitionSpec as P

CHANS = 128
FRAME = 512
TAPS = 8
BAND_START = 64
SPECTRA = 256
ITERS = 10


def window_table():
    index = jnp.arange(TAPS * FRAME, dtype=jnp.float32)
    offset = (index - TAPS * FRAME / 2 + 0.5) / FRAME
    taper = 0.5 - 0.5 * jnp.cos(2.0 * math.pi * (index + 0.5) / (TAPS * FRAME))
    return (jnp.sinc(offset) * taper).reshape(TAPS, FRAME)


def transform_table():
    sample = jnp.arange(FRAME, dtype=jnp.int32)
    channel = BAND_START + jnp.arange(CHANS, dtype=jnp.int32)
    angle = (sample[:, None] * channel[None, :] % FRAME).astype(jnp.float32) * (
        2.0 * math.pi / FRAME
    )
    return jnp.stack([jnp.cos(angle), -jnp.sin(angle)], axis=1).astype(jnp.bfloat16)


def transform_kernel(keep_ref, window_ref, table_ref, samples_ref, out_ref, wide_ref):
    group = samples_ref.shape[0]
    base = pl.program_id(0) * group
    scale = 1.0 / (64.0 * math.sqrt(FRAME))
    for item in range(group):
        wide_ref[0 : SPECTRA + TAPS - 1, :] = samples_ref[item].astype(jnp.float32)
        frames = window_ref[0:1, :] * wide_ref[0:SPECTRA, :]
        for tap in range(1, TAPS):
            frames = frames + window_ref[tap : tap + 1, :] * wide_ref[tap : tap + SPECTRA, :]
        result = lax.dot_general(
            table_ref[...], frames.astype(jnp.bfloat16), (((1,), (1,)), ((), ())),
            preferred_element_type=jnp.float32,
        )
        result = result * (scale * keep_ref[base + item])
        out_ref[:, item, :SPECTRA] = result[:CHANS].astype(out_ref.dtype)
        out_ref[:, item, SPECTRA:] = result[CHANS:].astype(out_ref.dtype)


def channelize(voltages, keep):
    window = window_table()
    table = transform_table()
    count = voltages.shape[0]
    samples = voltages.astype(jnp.bfloat16).reshape(count, SPECTRA + TAPS - 1, FRAME)
    table_t = jnp.transpose(table.reshape(FRAME, 2 * CHANS))
    group = 8
    return pl.pallas_call(
        transform_kernel,
        grid=(count // group,),
        in_specs=[
            pl.BlockSpec(memory_space=pltpu.SMEM),
            pl.BlockSpec((TAPS, FRAME), lambda g: (0, 0)),
            pl.BlockSpec((2 * CHANS, FRAME), lambda g: (0, 0)),
            pl.BlockSpec((group, SPECTRA + TAPS - 1, FRAME), lambda g: (g, 0, 0)),
        ],
        out_specs=pl.BlockSpec((CHANS, group, 2 * SPECTRA), lambda g: (0, g, 0)),
        out_shape=jax.ShapeDtypeStruct((CHANS, count, 2 * SPECTRA), jnp.bfloat16),
        scratch_shapes=[pltpu.VMEM((SPECTRA + 2 * TAPS, FRAME), jnp.float32)],
        cost_estimate=pl.CostEstimate(
            flops=2 * count * SPECTRA * FRAME * (2 * CHANS + TAPS),
            transcendentals=0,
            bytes_accessed=2 * count * (SPECTRA + TAPS) * FRAME + 2 * CHANS * count * 2 * SPECTRA,
        ),
    )(keep, window, table_t, samples)


def split3(value):
    high = value.astype(jnp.bfloat16)
    rest = value - high.astype(jnp.float32)
    mid = rest.astype(jnp.bfloat16)
    low = (rest - mid.astype(jnp.float32)).astype(jnp.bfloat16)
    return jnp.concatenate([high, mid, low], axis=-1)


def exact_dot(lhs, rhs_f32, dims):
    cols = rhs_f32.shape[-1]
    parts = lax.dot_general(
        lhs, split3(rhs_f32), (dims, ((), ())), preferred_element_type=jnp.float32
    )
    return parts[:, :cols] + parts[:, cols : 2 * cols] + parts[:, 2 * cols :]


def solve_gains(data, model_re, model_im):
    count = data.shape[0]

    def sweep(gain_re, gain_im):
        probe_re = gain_re * model_re - gain_im * model_im
        probe_im = gain_re * model_im + gain_im * model_re
        power = jnp.sum(probe_re * probe_re + probe_im * probe_im)
        half = exact_dot(data, jnp.stack([probe_re, probe_im], axis=1), ((0,), (0,)))
        u_re = half[:SPECTRA, 0] + half[SPECTRA:, 1]
        u_im = half[:SPECTRA, 1] - half[SPECTRA:, 0]
        mix = jnp.concatenate(
            [jnp.stack([u_re, u_im], axis=1), jnp.stack([-u_im, u_re], axis=1)], axis=0
        )
        product = exact_dot(data, mix, ((1,), (0,))) * (1.0 / SPECTRA)
        product_re = product[:, 0]
        product_im = product[:, 1]
        denominator = (model_re * model_re + model_im * model_im) * (power + 1e-06)
        new_re = (model_re * product_re + model_im * product_im) / denominator
        new_im = (model_re * product_im - model_im * product_re) / denominator
        return new_re, new_im

    def paired(step_index, carried):
        first_re, first_im = sweep(carried[0], carried[1])
        second_re, second_im = sweep(first_re, first_im)
        return (0.5 * (second_re + first_re), 0.5 * (second_im + first_im))

    start_re = jnp.ones((count,), jnp.float32)
    start_im = jnp.zeros((count,), jnp.float32)
    return lax.fori_loop(0, ITERS // 2, paired, (start_re, start_im))


def correlate_kernel(block_ref, rows_ref, cols_ref, out_ref):
    dims = (((1,), (1,)), ((), ()))
    rows_re = rows_ref[0, :, :SPECTRA]
    rows_im = rows_ref[0, :, SPECTRA:]
    cols_re = cols_ref[0, :, :SPECTRA]
    cols_im = cols_ref[0, :, SPECTRA:]

    def dot(a, b):
        return lax.dot_general(a, b, dims, preferred_element_type=jnp.float32)

    real = dot(rows_re, cols_re) + dot(rows_im, cols_im)
    imag = dot(rows_im, cols_re) - dot(rows_re, cols_im)
    out_ref[0, 0] = (real * (1.0 / SPECTRA)).astype(out_ref.dtype)
    out_ref[1, 0] = (imag * (1.0 / SPECTRA)).astype(out_ref.dtype)


def correlate(data, scalars, row_count, out=None, total_chans=None, col_block=512):
    chans, inputs, width = data.shape
    total_chans = chans if total_chans is None else total_chans
    grid = (chans, inputs // col_block)
    in_specs = [
        pl.BlockSpec((1, row_count, width), lambda c, j, s: (c, s[0], 0)),
        pl.BlockSpec((1, col_block, width), lambda c, j, s: (c, j, 0)),
    ]
    operands = [scalars, data, data]
    aliases = {}
    if out is not None:
        in_specs.append(pl.BlockSpec(memory_space=pl.ANY))
        operands.append(out)
        aliases = {3: 0}
    spec = pltpu.PrefetchScalarGridSpec(
        num_scalar_prefetch=1,
        grid=grid,
        in_specs=in_specs,
        out_specs=pl.BlockSpec((2, 1, row_count, col_block), lambda c, j, s: (0, s[1] + c, 0, j)),
    )
    flops = 8 * chans * row_count * inputs * (width // 2)
    kernel = correlate_kernel if out is None else correlate_into_kernel
    return pl.pallas_call(
        kernel,
        grid_spec=spec,
        out_shape=jax.ShapeDtypeStruct((2, total_chans, row_count, inputs), jnp.bfloat16),
        input_output_aliases=aliases,
        cost_estimate=pl.CostEstimate(
            flops=flops,
            transcendentals=0,
            bytes_accessed=2 * chans * (inputs * width + row_count * width + 2 * row_count * inputs),
        ),
    )(*operands)


def correlate_into_kernel(block_ref, rows_ref, cols_ref, prev_ref, out_ref):
    correlate_kernel(block_ref, rows_ref, cols_ref, out_ref)


def shards(voltages, flags, model_amp, model_phase):
    keep = (1 - flags).astype(jnp.float32)
    input_count = voltages.shape[0]
    blk_count = lax.axis_size("blk")
    chan_count = lax.axis_size("chan")
    block_index = lax.axis_index("blk")
    pieces = 2
    part = input_count // pieces
    received = []
    for piece in range(pieces):
        spectra = channelize(
            voltages[piece * part : (piece + 1) * part], keep[piece * part : (piece + 1) * part]
        )
        spectra = spectra.reshape(chan_count, 2, 2, part, 2 * SPECTRA)
        send = jnp.broadcast_to(
            spectra[:, None], (chan_count, 2, 2, 2, part, 2 * SPECTRA)
        )
        send = send.reshape(chan_count * blk_count, 2, part, 2 * SPECTRA)
        send = jnp.swapaxes(send, 0, 1)
        received.append(
            lax.all_to_all(send, ("chan", "blk"), split_axis=1, concat_axis=1, tiled=True)
        )
    got = jnp.concatenate(received, axis=2)
    mine = got.reshape(2, -1, 2 * SPECTRA)
    all_inputs = mine.shape[1]
    row_count = all_inputs // blk_count
    core = block_index % 2
    level = block_index // 2
    theirs = lax.ppermute(mine, "blk", perm=[(b, b ^ 1) for b in range(blk_count)])
    local_chans = 4
    first = jnp.stack([block_index, 2 * core]).astype(jnp.int32)
    second = jnp.stack([block_index, 2 - 2 * core]).astype(jnp.int32)
    visibility = correlate(mine, first, row_count, total_chans=local_chans)
    visibility = correlate(theirs, second, row_count, out=visibility, total_chans=local_chans)

    data = lax.dynamic_index_in_dim(mine, level, 0, keepdims=False)
    solve = 2 * core + level
    amp = lax.dynamic_index_in_dim(model_amp, solve, 0, keepdims=False)
    phase = lax.dynamic_index_in_dim(model_phase, solve, 0, keepdims=False)
    full_re = amp * jnp.cos(phase)
    full_im = amp * jnp.sin(phase)
    solved = jnp.stack(solve_gains(data, full_re, full_im))
    owners = solved.reshape(2, chan_count * blk_count, 1, input_count)
    gains = lax.all_to_all(owners, ("chan", "blk"), split_axis=1, concat_axis=1, tiled=True)
    gains = gains.reshape(2, chan_count, 2, 2, input_count)
    gains = jnp.swapaxes(gains, 2, 3).reshape(2, -1, input_count)
    return (visibility, gains)


def solution(mesh):
    return jax.shard_map(
        shards,
        mesh=mesh,
        in_specs=(P(("chan", "blk"), None), P(("chan", "blk")), P("chan", None), P("chan", None)),
        out_specs=(P(None, "chan", "blk", None), P(None, None, ("chan", "blk"))),
        check_vma=False,
    )
```

```python
import math

import jax
import jax.numpy as jnp
from jax import lax
from jax.experimental import pallas as pl
from jax.experimental.pallas import tpu as pltpu
from jax.sharding import PartitionSpec as P

CHANS = 128
FRAME = 512
TAPS = 8
BAND_START = 64
SPECTRA = 256
ITERS = 10


def window_table():
    index = jnp.arange(TAPS * FRAME, dtype=jnp.float32)
    offset = (index - TAPS * FRAME / 2 + 0.5) / FRAME
    taper = 0.5 - 0.5 * jnp.cos(2.0 * math.pi * (index + 0.5) / (TAPS * FRAME))
    return (jnp.sinc(offset) * taper).reshape(TAPS, FRAME)


def transform_table():
    sample = jnp.arange(FRAME, dtype=jnp.int32)
    channel = BAND_START + jnp.arange(CHANS, dtype=jnp.int32)
    angle = (sample[:, None] * channel[None, :] % FRAME).astype(jnp.float32) * (
        2.0 * math.pi / FRAME
    )
    return jnp.stack([jnp.cos(angle), -jnp.sin(angle)], axis=1).astype(jnp.bfloat16)


def transform_kernel(keep_ref, window_ref, table_ref, samples_ref, out_ref, wide_ref):
    group = samples_ref.shape[0]
    base = pl.program_id(0) * group
    scale = 1.0 / (64.0 * math.sqrt(FRAME))
    for item in range(group):
        wide_ref[0 : SPECTRA + TAPS - 1, :] = samples_ref[item].astype(jnp.float32)
        frames = window_ref[0:1, :] * wide_ref[0:SPECTRA, :]
        for tap in range(1, TAPS):
            frames = frames + window_ref[tap : tap + 1, :] * wide_ref[tap : tap + SPECTRA, :]
        result = lax.dot_general(
            table_ref[...], frames.astype(jnp.bfloat16), (((1,), (1,)), ((), ())),
            preferred_element_type=jnp.float32,
        )
        result = result * (scale * keep_ref[base + item])
        out_ref[:, item, :SPECTRA] = result[:CHANS].astype(out_ref.dtype)
        out_ref[:, item, SPECTRA:] = result[CHANS:].astype(out_ref.dtype)


def channelize(voltages, keep):
    window = window_table()
    table = transform_table()
    count = voltages.shape[0]
    samples = voltages.astype(jnp.bfloat16).reshape(count, SPECTRA + TAPS - 1, FRAME)
    table_t = jnp.transpose(table.reshape(FRAME, 2 * CHANS))
    group = 8
    return pl.pallas_call(
        transform_kernel,
        grid=(count // group,),
        in_specs=[
            pl.BlockSpec(memory_space=pltpu.SMEM),
            pl.BlockSpec((TAPS, FRAME), lambda g: (0, 0)),
            pl.BlockSpec((2 * CHANS, FRAME), lambda g: (0, 0)),
            pl.BlockSpec((group, SPECTRA + TAPS - 1, FRAME), lambda g: (g, 0, 0)),
        ],
        out_specs=pl.BlockSpec((CHANS, group, 2 * SPECTRA), lambda g: (0, g, 0)),
        out_shape=jax.ShapeDtypeStruct((CHANS, count, 2 * SPECTRA), jnp.bfloat16),
        scratch_shapes=[pltpu.VMEM((SPECTRA + 2 * TAPS, FRAME), jnp.float32)],
        cost_estimate=pl.CostEstimate(
            flops=2 * count * SPECTRA * FRAME * (2 * CHANS + TAPS),
            transcendentals=0,
            bytes_accessed=2 * count * (SPECTRA + TAPS) * FRAME + 2 * CHANS * count * 2 * SPECTRA,
        ),
    )(keep, window, table_t, samples)


def split3(value):
    high = value.astype(jnp.bfloat16)
    rest = value - high.astype(jnp.float32)
    mid = rest.astype(jnp.bfloat16)
    low = (rest - mid.astype(jnp.float32)).astype(jnp.bfloat16)
    return jnp.concatenate([high, mid, low], axis=-1)


def exact_dot(lhs, rhs_f32, dims):
    cols = rhs_f32.shape[-1]
    parts = lax.dot_general(
        lhs, split3(rhs_f32), (dims, ((), ())), preferred_element_type=jnp.float32
    )
    return parts[:, :cols] + parts[:, cols : 2 * cols] + parts[:, 2 * cols :]


def solve_gains(data, model_re, model_im):
    count = data.shape[0]

    def sweep(gain_re, gain_im):
        probe_re = gain_re * model_re - gain_im * model_im
        probe_im = gain_re * model_im + gain_im * model_re
        power = jnp.sum(probe_re * probe_re + probe_im * probe_im)
        half = exact_dot(data, jnp.stack([probe_re, probe_im], axis=1), ((0,), (0,)))
        u_re = half[:SPECTRA, 0] + half[SPECTRA:, 1]
        u_im = half[:SPECTRA, 1] - half[SPECTRA:, 0]
        mix = jnp.concatenate(
            [jnp.stack([u_re, u_im], axis=1), jnp.stack([-u_im, u_re], axis=1)], axis=0
        )
        product = exact_dot(data, mix, ((1,), (0,))) * (1.0 / SPECTRA)
        product_re = product[:, 0]
        product_im = product[:, 1]
        denominator = (model_re * model_re + model_im * model_im) * (power + 1e-06)
        new_re = (model_re * product_re + model_im * product_im) / denominator
        new_im = (model_re * product_im - model_im * product_re) / denominator
        return new_re, new_im

    def paired(step_index, carried):
        first_re, first_im = sweep(carried[0], carried[1])
        second_re, second_im = sweep(first_re, first_im)
        return (0.5 * (second_re + first_re), 0.5 * (second_im + first_im))

    start_re = jnp.ones((count,), jnp.float32)
    start_im = jnp.zeros((count,), jnp.float32)
    return lax.fori_loop(0, ITERS // 2, paired, (start_re, start_im))


def correlate_kernel(block_ref, rows_ref, cols_ref, out_ref, turned_ref):
    width = rows_ref.shape[-1]
    rows = rows_ref[:, 0].reshape(-1, width)

    @pl.when(pl.program_id(1) == 0)
    def _():
        turned_ref[:, :SPECTRA] = rows[:, SPECTRA:]
        turned_ref[:, SPECTRA:] = -rows[:, :SPECTRA]

    cols = cols_ref[:, 0].reshape(-1, width)
    dims = (((1,), (1,)), ((), ()))
    real = lax.dot_general(rows, cols, dims, preferred_element_type=jnp.float32)
    imag = lax.dot_general(turned_ref[...], cols, dims, preferred_element_type=jnp.float32)
    out_ref[0, 0] = (real * (1.0 / SPECTRA)).astype(out_ref.dtype)
    out_ref[1, 0] = (imag * (1.0 / SPECTRA)).astype(out_ref.dtype)


def correlate_into_kernel(block_ref, rows_ref, cols_ref, prev_ref, out_ref, turned_ref):
    correlate_kernel(block_ref, rows_ref, cols_ref, out_ref, turned_ref)


def correlate(data, scalars, row_count, out=None, total_chans=None, col_block=512):
    devices, chans, per, width = data.shape
    inputs = devices * per
    total_chans = chans if total_chans is None else total_chans
    grid = (chans, inputs // col_block)
    row_devices = row_count // per
    col_devices = col_block // per
    in_specs = [
        pl.BlockSpec((row_devices, 1, per, width), lambda c, j, s: (s[0], c, 0, 0)),
        pl.BlockSpec((col_devices, 1, per, width), lambda c, j, s: (j, c, 0, 0)),
    ]
    operands = [scalars, data, data]
    aliases = {}
    if out is not None:
        in_specs.append(pl.BlockSpec(memory_space=pl.ANY))
        operands.append(out)
        aliases = {3: 0}
    spec = pltpu.PrefetchScalarGridSpec(
        num_scalar_prefetch=1,
        grid=grid,
        in_specs=in_specs,
        out_specs=pl.BlockSpec((2, 1, row_count, col_block), lambda c, j, s: (0, s[1] + c, 0, j)),
        scratch_shapes=[pltpu.VMEM((row_count, width), data.dtype)],
    )
    flops = 8 * chans * row_count * inputs * (width // 2)
    kernel = correlate_kernel if out is None else correlate_into_kernel
    return pl.pallas_call(
        kernel,
        grid_spec=spec,
        out_shape=jax.ShapeDtypeStruct((2, total_chans, row_count, inputs), jnp.bfloat16),
        input_output_aliases=aliases,
        cost_estimate=pl.CostEstimate(
            flops=flops,
            transcendentals=0,
            bytes_accessed=2 * chans * (inputs * width + row_count * width + 2 * row_count * inputs),
        ),
    )(*operands)


def shards(voltages, flags, model_amp, model_phase):
    keep = (1 - flags).astype(jnp.float32)
    input_count = voltages.shape[0]
    spectra = channelize(voltages, keep)
    blk_count = lax.axis_size("blk")
    chan_count = lax.axis_size("chan")
    block_index = lax.axis_index("blk")
    spectra = spectra.reshape(chan_count, 2, 2, input_count, 2 * SPECTRA)
    send = jnp.broadcast_to(
        spectra[:, None], (chan_count, 2, 2, 2, input_count, 2 * SPECTRA)
    )
    send = send.reshape(chan_count * blk_count, 2, input_count, 2 * SPECTRA)
    mine = lax.all_to_all(send, ("chan", "blk"), split_axis=0, concat_axis=0, tiled=True)
    all_inputs = mine.shape[0] * input_count
    row_count = all_inputs // blk_count
    core = block_index % 2
    level = block_index // 2
    theirs = lax.ppermute(mine, "blk", perm=[(b, b ^ 1) for b in range(blk_count)])
    local_chans = 4
    first = jnp.stack([block_index, 2 * core]).astype(jnp.int32)
    second = jnp.stack([block_index, 2 - 2 * core]).astype(jnp.int32)
    visibility = correlate(mine, first, row_count, total_chans=local_chans)
    visibility = correlate(theirs, second, row_count, out=visibility, total_chans=local_chans)

    data = lax.dynamic_index_in_dim(mine, level, 1, keepdims=False).reshape(all_inputs, -1)
    solve = 2 * core + level
    amp = lax.dynamic_index_in_dim(model_amp, solve, 0, keepdims=False)
    phase = lax.dynamic_index_in_dim(model_phase, solve, 0, keepdims=False)
    full_re = amp * jnp.cos(phase)
    full_im = amp * jnp.sin(phase)
    solved = jnp.stack(solve_gains(data, full_re, full_im))
    owners = solved.reshape(2, chan_count * blk_count, 1, input_count)
    gains = lax.all_to_all(owners, ("chan", "blk"), split_axis=1, concat_axis=1, tiled=True)
    gains = gains.reshape(2, chan_count, 2, 2, input_count)
    gains = jnp.swapaxes(gains, 2, 3).reshape(2, -1, input_count)
    return (visibility, gains)


def solution(mesh):
    return jax.shard_map(
        shards,
        mesh=mesh,
        in_specs=(P(("chan", "blk"), None), P(("chan", "blk")), P("chan", None), P("chan", None)),
        out_specs=(P(None, "chan", "blk", None), P(None, None, ("chan", "blk"))),
        check_vma=False,
    )
```

```python
import math

import jax
import jax.numpy as jnp
from jax import lax
from jax.experimental import pallas as pl
from jax.experimental.pallas import tpu as pltpu
from jax.sharding import PartitionSpec as P

CHANS = 128
FRAME = 512
TAPS = 8
BAND_START = 64
SPECTRA = 256
ITERS = 10


def window_table():
    index = jnp.arange(TAPS * FRAME, dtype=jnp.float32)
    offset = (index - TAPS * FRAME / 2 + 0.5) / FRAME
    taper = 0.5 - 0.5 * jnp.cos(2.0 * math.pi * (index + 0.5) / (TAPS * FRAME))
    return (jnp.sinc(offset) * taper).reshape(TAPS, FRAME)


def transform_table():
    sample = jnp.arange(FRAME, dtype=jnp.int32)
    channel = BAND_START + jnp.arange(CHANS, dtype=jnp.int32)
    angle = (sample[:, None] * channel[None, :] % FRAME).astype(jnp.float32) * (
        2.0 * math.pi / FRAME
    )
    return jnp.stack([jnp.cos(angle), -jnp.sin(angle)], axis=1).astype(jnp.bfloat16)


def transform_kernel(keep_ref, window_ref, table_ref, samples_ref, out_ref, wide_ref):
    group = samples_ref.shape[0]
    base = pl.program_id(0) * group
    scale = 1.0 / (64.0 * math.sqrt(FRAME))
    for item in range(group):
        wide_ref[0 : SPECTRA + TAPS - 1, :] = samples_ref[item].astype(jnp.float32)
        frames = window_ref[0:1, :] * wide_ref[0:SPECTRA, :]
        for tap in range(1, TAPS):
            frames = frames + window_ref[tap : tap + 1, :] * wide_ref[tap : tap + SPECTRA, :]
        result = lax.dot_general(
            table_ref[...], frames.astype(jnp.bfloat16), (((1,), (1,)), ((), ())),
            preferred_element_type=jnp.float32,
        )
        result = result * (scale * keep_ref[base + item])
        out_ref[:, item, :SPECTRA] = result[:CHANS].astype(out_ref.dtype)
        out_ref[:, item, SPECTRA:] = result[CHANS:].astype(out_ref.dtype)


def channelize(voltages, keep):
    window = window_table()
    table = transform_table()
    count = voltages.shape[0]
    samples = voltages.reshape(count, SPECTRA + TAPS - 1, FRAME)
    table_t = jnp.transpose(table.reshape(FRAME, 2 * CHANS))
    group = 8
    return pl.pallas_call(
        transform_kernel,
        grid=(count // group,),
        in_specs=[
            pl.BlockSpec(memory_space=pltpu.SMEM),
            pl.BlockSpec((TAPS, FRAME), lambda g: (0, 0)),
            pl.BlockSpec((2 * CHANS, FRAME), lambda g: (0, 0)),
            pl.BlockSpec((group, SPECTRA + TAPS - 1, FRAME), lambda g: (g, 0, 0)),
        ],
        out_specs=pl.BlockSpec((CHANS, group, 2 * SPECTRA), lambda g: (0, g, 0)),
        out_shape=jax.ShapeDtypeStruct((CHANS, count, 2 * SPECTRA), jnp.bfloat16),
        scratch_shapes=[pltpu.VMEM((SPECTRA + 2 * TAPS, FRAME), jnp.float32)],
        cost_estimate=pl.CostEstimate(
            flops=2 * count * SPECTRA * FRAME * (2 * CHANS + TAPS),
            transcendentals=0,
            bytes_accessed=4 * count * (SPECTRA + TAPS) * FRAME + 2 * CHANS * count * 2 * SPECTRA,
        ),
    )(keep, window, table_t, samples)


def split3(value):
    high = value.astype(jnp.bfloat16)
    rest = value - high.astype(jnp.float32)
    mid = rest.astype(jnp.bfloat16)
    low = (rest - mid.astype(jnp.float32)).astype(jnp.bfloat16)
    return jnp.concatenate([high, mid, low], axis=-1)


def exact_dot(lhs, rhs_f32, dims):
    cols = rhs_f32.shape[-1]
    parts = lax.dot_general(
        lhs, split3(rhs_f32), (dims, ((), ())), preferred_element_type=jnp.float32
    )
    return parts[:, :cols] + parts[:, cols : 2 * cols] + parts[:, 2 * cols :]


def solve_gains(data, model_re, model_im):
    count = data.shape[0]

    def sweep(gain_re, gain_im):
        probe_re = gain_re * model_re - gain_im * model_im
        probe_im = gain_re * model_im + gain_im * model_re
        power = jnp.sum(probe_re * probe_re + probe_im * probe_im)
        half = exact_dot(data, jnp.stack([probe_re, probe_im], axis=1), ((0,), (0,)))
        u_re = half[:SPECTRA, 0] + half[SPECTRA:, 1]
        u_im = half[:SPECTRA, 1] - half[SPECTRA:, 0]
        mix = jnp.concatenate(
            [jnp.stack([u_re, u_im], axis=1), jnp.stack([-u_im, u_re], axis=1)], axis=0
        )
        product = exact_dot(data, mix, ((1,), (0,))) * (1.0 / SPECTRA)
        product_re = product[:, 0]
        product_im = product[:, 1]
        denominator = (model_re * model_re + model_im * model_im) * (power + 1e-06)
        new_re = (model_re * product_re + model_im * product_im) / denominator
        new_im = (model_re * product_im - model_im * product_re) / denominator
        return new_re, new_im

    def paired(step_index, carried):
        first_re, first_im = sweep(carried[0], carried[1])
        second_re, second_im = sweep(first_re, first_im)
        return (0.5 * (second_re + first_re), 0.5 * (second_im + first_im))

    start_re = jnp.ones((count,), jnp.float32)
    start_im = jnp.zeros((count,), jnp.float32)
    return lax.fori_loop(0, ITERS // 2, paired, (start_re, start_im), unroll=True)


def correlate_kernel(block_ref, rows_ref, cols_ref, out_ref, turned_ref):
    width = rows_ref.shape[-1]
    rows = rows_ref[:, 0].reshape(-1, width)

    @pl.when(pl.program_id(1) == 0)
    def _():
        turned_ref[:, :SPECTRA] = rows[:, SPECTRA:]
        turned_ref[:, SPECTRA:] = -rows[:, :SPECTRA]

    cols = cols_ref[:, 0].reshape(-1, width)
    dims = (((1,), (1,)), ((), ()))
    real = lax.dot_general(rows, cols, dims, preferred_element_type=jnp.float32)
    imag = lax.dot_general(turned_ref[...], cols, dims, preferred_element_type=jnp.float32)
    out_ref[0, 0] = (real * (1.0 / SPECTRA)).astype(out_ref.dtype)
    out_ref[1, 0] = (imag * (1.0 / SPECTRA)).astype(out_ref.dtype)


def correlate_into_kernel(block_ref, rows_ref, cols_ref, prev_ref, out_ref, turned_ref):
    correlate_kernel(block_ref, rows_ref, cols_ref, out_ref, turned_ref)


def correlate(data, scalars, row_count, out=None, total_chans=None, col_block=512):
    devices, chans, per, width = data.shape
    inputs = devices * per
    total_chans = chans if total_chans is None else total_chans
    grid = (chans, inputs // col_block)
    row_devices = row_count // per
    col_devices = col_block // per
    in_specs = [
        pl.BlockSpec((row_devices, 1, per, width), lambda c, j, s: (s[0], c, 0, 0)),
        pl.BlockSpec((col_devices, 1, per, width), lambda c, j, s: (j, c, 0, 0)),
    ]
    operands = [scalars, data, data]
    aliases = {}
    if out is not None:
        in_specs.append(pl.BlockSpec(memory_space=pl.ANY))
        operands.append(out)
        aliases = {3: 0}
    spec = pltpu.PrefetchScalarGridSpec(
        num_scalar_prefetch=1,
        grid=grid,
        in_specs=in_specs,
        out_specs=pl.BlockSpec((2, 1, row_count, col_block), lambda c, j, s: (0, s[1] + c, 0, j)),
        scratch_shapes=[pltpu.VMEM((row_count, width), data.dtype)],
    )
    flops = 8 * chans * row_count * inputs * (width // 2)
    kernel = correlate_kernel if out is None else correlate_into_kernel
    return pl.pallas_call(
        kernel,
        grid_spec=spec,
        out_shape=jax.ShapeDtypeStruct((2, total_chans, row_count, inputs), jnp.bfloat16),
        input_output_aliases=aliases,
        cost_estimate=pl.CostEstimate(
            flops=flops,
            transcendentals=0,
            bytes_accessed=2 * chans * (inputs * width + row_count * width + 2 * row_count * inputs),
        ),
    )(*operands)


def shards(voltages, flags, model_amp, model_phase):
    keep = (1 - flags).astype(jnp.float32)
    input_count = voltages.shape[0]
    spectra = channelize(voltages, keep)
    blk_count = lax.axis_size("blk")
    chan_count = lax.axis_size("chan")
    block_index = lax.axis_index("blk")
    spectra = spectra.reshape(chan_count, 2, 2, input_count, 2 * SPECTRA)
    send = jnp.broadcast_to(
        spectra[:, None], (chan_count, 2, 2, 2, input_count, 2 * SPECTRA)
    )
    send = send.reshape(chan_count * blk_count, 2, input_count, 2 * SPECTRA)
    mine = lax.all_to_all(send, ("chan", "blk"), split_axis=0, concat_axis=0, tiled=True)
    all_inputs = mine.shape[0] * input_count
    row_count = all_inputs // blk_count
    core = block_index % 2
    level = block_index // 2
    theirs = lax.ppermute(mine, "blk", perm=[(b, b ^ 1) for b in range(blk_count)])
    local_chans = 4
    first = jnp.stack([block_index, 2 * core]).astype(jnp.int32)
    second = jnp.stack([block_index, 2 - 2 * core]).astype(jnp.int32)
    visibility = correlate(mine, first, row_count, total_chans=local_chans)
    visibility = correlate(theirs, second, row_count, out=visibility, total_chans=local_chans)

    data = lax.dynamic_index_in_dim(mine, level, 1, keepdims=False).reshape(all_inputs, -1)
    solve = 2 * core + level
    amp = lax.dynamic_index_in_dim(model_amp, solve, 0, keepdims=False)
    phase = lax.dynamic_index_in_dim(model_phase, solve, 0, keepdims=False)
    full_re = amp * jnp.cos(phase)
    full_im = amp * jnp.sin(phase)
    solved = jnp.stack(solve_gains(data, full_re, full_im))
    owners = solved.reshape(2, chan_count * blk_count, 1, input_count)
    gains = lax.all_to_all(owners, ("chan", "blk"), split_axis=1, concat_axis=1, tiled=True)
    gains = gains.reshape(2, chan_count, 2, 2, input_count)
    gains = jnp.swapaxes(gains, 2, 3).reshape(2, -1, input_count)
    return (visibility, gains)


def solution(mesh):
    return jax.shard_map(
        shards,
        mesh=mesh,
        in_specs=(P(("chan", "blk"), None), P(("chan", "blk")), P("chan", None), P("chan", None)),
        out_specs=(P(None, "chan", "blk", None), P(None, None, ("chan", "blk"))),
        check_vma=False,
    )
```

```python
import math

import jax
import jax.numpy as jnp
from jax import lax
from jax.experimental import pallas as pl
from jax.experimental.pallas import tpu as pltpu
from jax.sharding import PartitionSpec as P

CHANS = 128
FRAME = 512
TAPS = 8
BAND_START = 64
SPECTRA = 256
ITERS = 10


def window_table():
    index = jnp.arange(TAPS * FRAME, dtype=jnp.float32)
    offset = (index - TAPS * FRAME / 2 + 0.5) / FRAME
    taper = 0.5 - 0.5 * jnp.cos(2.0 * math.pi * (index + 0.5) / (TAPS * FRAME))
    return (jnp.sinc(offset) * taper).reshape(TAPS, FRAME)


def transform_table():
    sample = jnp.arange(FRAME, dtype=jnp.int32)
    channel = BAND_START + jnp.arange(CHANS, dtype=jnp.int32)
    angle = (sample[:, None] * channel[None, :] % FRAME).astype(jnp.float32) * (
        2.0 * math.pi / FRAME
    )
    return jnp.stack([jnp.cos(angle), -jnp.sin(angle)], axis=1).astype(jnp.bfloat16)


def transform_kernel(keep_ref, window_ref, table_ref, samples_ref, out_ref, wide_ref):
    group = samples_ref.shape[0]
    base = pl.program_id(0) * group
    scale = 1.0 / (64.0 * math.sqrt(FRAME))
    for item in range(group):
        wide_ref[0 : SPECTRA + TAPS - 1, :] = samples_ref[item].astype(jnp.float32)
        frames = window_ref[0:1, :] * wide_ref[0:SPECTRA, :]
        for tap in range(1, TAPS):
            frames = frames + window_ref[tap : tap + 1, :] * wide_ref[tap : tap + SPECTRA, :]
        result = lax.dot_general(
            table_ref[...], frames.astype(jnp.bfloat16), (((1,), (1,)), ((), ())),
            preferred_element_type=jnp.float32,
        )
        result = result * (scale * keep_ref[base + item])
        out_ref[:, item, :SPECTRA] = result[:CHANS].astype(out_ref.dtype)
        out_ref[:, item, SPECTRA:] = result[CHANS:].astype(out_ref.dtype)


def channelize(voltages, keep):
    window = window_table()
    table = transform_table()
    count = voltages.shape[0]
    samples = voltages.reshape(count, SPECTRA + TAPS - 1, FRAME)
    table_t = jnp.transpose(table.reshape(FRAME, 2 * CHANS))
    group = 8
    return pl.pallas_call(
        transform_kernel,
        grid=(count // group,),
        in_specs=[
            pl.BlockSpec(memory_space=pltpu.SMEM),
            pl.BlockSpec((TAPS, FRAME), lambda g: (0, 0)),
            pl.BlockSpec((2 * CHANS, FRAME), lambda g: (0, 0)),
            pl.BlockSpec((group, SPECTRA + TAPS - 1, FRAME), lambda g: (g, 0, 0)),
        ],
        out_specs=pl.BlockSpec((CHANS, group, 2 * SPECTRA), lambda g: (0, g, 0)),
        out_shape=jax.ShapeDtypeStruct((CHANS, count, 2 * SPECTRA), jnp.bfloat16),
        scratch_shapes=[pltpu.VMEM((SPECTRA + 2 * TAPS, FRAME), jnp.float32)],
        cost_estimate=pl.CostEstimate(
            flops=2 * count * SPECTRA * FRAME * (2 * CHANS + TAPS),
            transcendentals=0,
            bytes_accessed=4 * count * (SPECTRA + TAPS) * FRAME + 2 * CHANS * count * 2 * SPECTRA,
        ),
    )(keep, window, table_t, samples)


def split3(value):
    high = value.astype(jnp.bfloat16)
    rest = value - high.astype(jnp.float32)
    mid = rest.astype(jnp.bfloat16)
    low = (rest - mid.astype(jnp.float32)).astype(jnp.bfloat16)
    return jnp.concatenate([high, mid, low], axis=-1)


def exact_dot(lhs, rhs_f32, dims):
    cols = rhs_f32.shape[-1]
    parts = lax.dot_general(
        lhs, split3(rhs_f32), (dims, ((), ())), preferred_element_type=jnp.float32
    )
    return parts[:, :cols] + parts[:, cols : 2 * cols] + parts[:, 2 * cols :]


def solve_gains(data, model_re, model_im):
    count = data.shape[0]

    def sweep(gain_re, gain_im):
        probe_re = gain_re * model_re - gain_im * model_im
        probe_im = gain_re * model_im + gain_im * model_re
        power = jnp.sum(probe_re * probe_re + probe_im * probe_im)
        half = exact_dot(data, jnp.stack([probe_re, probe_im], axis=1), ((0,), (0,)))
        u_re = half[:SPECTRA, 0] + half[SPECTRA:, 1]
        u_im = half[:SPECTRA, 1] - half[SPECTRA:, 0]
        mix = jnp.concatenate(
            [jnp.stack([u_re, u_im], axis=1), jnp.stack([-u_im, u_re], axis=1)], axis=0
        )
        product = exact_dot(data, mix, ((1,), (0,))) * (1.0 / SPECTRA)
        product_re = product[:, 0]
        product_im = product[:, 1]
        denominator = (model_re * model_re + model_im * model_im) * (power + 1e-06)
        new_re = (model_re * product_re + model_im * product_im) / denominator
        new_im = (model_re * product_im - model_im * product_re) / denominator
        return new_re, new_im

    def paired(step_index, carried):
        first_re, first_im = sweep(carried[0], carried[1])
        second_re, second_im = sweep(first_re, first_im)
        return (0.5 * (second_re + first_re), 0.5 * (second_im + first_im))

    start_re = jnp.ones((count,), jnp.float32)
    start_im = jnp.zeros((count,), jnp.float32)
    return lax.fori_loop(0, ITERS // 2, paired, (start_re, start_im), unroll=True)


def correlate_kernel(block_ref, rows_ref, cols_ref, out_ref, turned_ref):
    width = rows_ref.shape[-1]
    rows = rows_ref[:, 0].reshape(-1, width)

    @pl.when(pl.program_id(1) == 0)
    def _():
        turned_ref[:, :SPECTRA] = rows[:, SPECTRA:]
        turned_ref[:, SPECTRA:] = -rows[:, :SPECTRA]

    cols = cols_ref[:, 0].reshape(-1, width)
    dims = (((1,), (1,)), ((), ()))
    real = lax.dot_general(rows, cols, dims, preferred_element_type=jnp.float32)
    imag = lax.dot_general(turned_ref[...], cols, dims, preferred_element_type=jnp.float32)
    out_ref[0, 0] = (real * (1.0 / SPECTRA)).astype(out_ref.dtype)
    out_ref[1, 0] = (imag * (1.0 / SPECTRA)).astype(out_ref.dtype)


def correlate_into_kernel(block_ref, rows_ref, cols_ref, prev_ref, out_ref, turned_ref):
    correlate_kernel(block_ref, rows_ref, cols_ref, out_ref, turned_ref)


def correlate(data, scalars, row_count, out=None, total_chans=None, col_block=512):
    devices, chans, per, width = data.shape
    inputs = devices * per
    total_chans = chans if total_chans is None else total_chans
    grid = (chans, inputs // col_block)
    row_devices = row_count // per
    col_devices = col_block // per
    in_specs = [
        pl.BlockSpec((row_devices, 1, per, width), lambda c, j, s: (s[0], c, 0, 0)),
        pl.BlockSpec((col_devices, 1, per, width), lambda c, j, s: (j, c, 0, 0)),
    ]
    operands = [scalars, data, data]
    aliases = {}
    if out is not None:
        in_specs.append(pl.BlockSpec(memory_space=pl.ANY))
        operands.append(out)
        aliases = {3: 0}
    spec = pltpu.PrefetchScalarGridSpec(
        num_scalar_prefetch=1,
        grid=grid,
        in_specs=in_specs,
        out_specs=pl.BlockSpec((2, 1, row_count, col_block), lambda c, j, s: (0, s[1] + c, 0, j)),
        scratch_shapes=[pltpu.VMEM((row_count, width), data.dtype)],
    )
    flops = 8 * chans * row_count * inputs * (width // 2)
    kernel = correlate_kernel if out is None else correlate_into_kernel
    return pl.pallas_call(
        kernel,
        grid_spec=spec,
        out_shape=jax.ShapeDtypeStruct((2, total_chans, row_count, inputs), jnp.bfloat16),
        input_output_aliases=aliases,
        cost_estimate=pl.CostEstimate(
            flops=flops,
            transcendentals=0,
            bytes_accessed=2 * chans * (inputs * width + row_count * width + 2 * row_count * inputs),
        ),
    )(*operands)


def shards(voltages, flags, model_amp, model_phase):
    keep = (1 - flags).astype(jnp.float32)
    input_count = voltages.shape[0]
    spectra = channelize(voltages, keep)
    blk_count = lax.axis_size("blk")
    chan_count = lax.axis_size("chan")
    block_index = lax.axis_index("blk")
    spectra = spectra.reshape(chan_count, 2, 2, input_count, 2 * SPECTRA)
    first_send = jnp.swapaxes(spectra, 1, 2)
    second_send = jnp.swapaxes(spectra[:, :, ::-1], 1, 2)
    devices = chan_count * blk_count

    def turn(send):
        send = send.reshape(devices, input_count, 2 * SPECTRA)
        return lax.all_to_all(send, ("chan", "blk"), split_axis=0, concat_axis=0, tiled=True)

    own = turn(first_send)
    all_inputs = devices * input_count
    row_count = all_inputs // blk_count
    core = block_index % 2
    level = block_index // 2
    swap = [(b, b ^ 1) for b in range(blk_count)]
    own_partner = lax.ppermute(own, "blk", perm=swap)

    solve = 2 * core + level
    amp = lax.dynamic_index_in_dim(model_amp, solve, 0, keepdims=False)
    phase = lax.dynamic_index_in_dim(model_phase, solve, 0, keepdims=False)
    full_re = amp * jnp.cos(phase)
    full_im = amp * jnp.sin(phase)
    other = turn(second_send)
    other_partner = lax.ppermute(other, "blk", perm=swap)
    solved = jnp.stack(solve_gains(own.reshape(all_inputs, -1), full_re, full_im))
    owners = solved.reshape(2, devices, 1, input_count)
    gains = lax.all_to_all(owners, ("chan", "blk"), split_axis=1, concat_axis=1, tiled=True)
    gains = gains.reshape(2, chan_count, 2, 2, input_count)
    gains = jnp.swapaxes(gains, 2, 3).reshape(2, -1, input_count)

    local_chans = 4
    shape = (devices, 1, input_count, 2 * SPECTRA)
    visibility = None
    for data, chan in (
        (own, 2 * core + level),
        (other, 2 * core + 1 - level),
        (own_partner, 2 - 2 * core + level),
        (other_partner, 3 - 2 * core - level),
    ):
        scalars = jnp.stack([block_index, chan]).astype(jnp.int32)
        visibility = correlate(
            data.reshape(shape), scalars, row_count, out=visibility, total_chans=local_chans
        )
    return (visibility, gains)


def solution(mesh):
    return jax.shard_map(
        shards,
        mesh=mesh,
        in_specs=(P(("chan", "blk"), None), P(("chan", "blk")), P("chan", None), P("chan", None)),
        out_specs=(P(None, "chan", "blk", None), P(None, None, ("chan", "blk"))),
        check_vma=False,
    )
```

```python
import math

import jax
import jax.numpy as jnp
from jax import lax
from jax.experimental import pallas as pl
from jax.experimental.pallas import tpu as pltpu
from jax.sharding import PartitionSpec as P

CHANS = 128
FRAME = 512
TAPS = 8
BAND_START = 64
SPECTRA = 256
ITERS = 10


def window_table():
    index = jnp.arange(TAPS * FRAME, dtype=jnp.float32)
    offset = (index - TAPS * FRAME / 2 + 0.5) / FRAME
    taper = 0.5 - 0.5 * jnp.cos(2.0 * math.pi * (index + 0.5) / (TAPS * FRAME))
    return (jnp.sinc(offset) * taper).reshape(TAPS, FRAME)


def transform_table():
    sample = jnp.arange(FRAME, dtype=jnp.int32)
    channel = BAND_START + jnp.arange(CHANS, dtype=jnp.int32)
    angle = (sample[:, None] * channel[None, :] % FRAME).astype(jnp.float32) * (
        2.0 * math.pi / FRAME
    )
    return jnp.stack([jnp.cos(angle), -jnp.sin(angle)], axis=1).astype(jnp.bfloat16)


def transform_kernel(keep_ref, window_ref, table_ref, samples_ref, out_ref, wide_ref):
    group = samples_ref.shape[0]
    base = pl.program_id(0) * group
    scale = 1.0 / (64.0 * math.sqrt(FRAME))
    for item in range(group):
        wide_ref[0 : SPECTRA + TAPS - 1, :] = samples_ref[item].astype(jnp.float32)
        frames = window_ref[0:1, :] * wide_ref[0:SPECTRA, :]
        for tap in range(1, TAPS):
            frames = frames + window_ref[tap : tap + 1, :] * wide_ref[tap : tap + SPECTRA, :]
        result = lax.dot_general(
            table_ref[...], frames.astype(jnp.bfloat16), (((1,), (1,)), ((), ())),
            preferred_element_type=jnp.float32,
        )
        result = result * (scale * keep_ref[base + item])
        out_ref[:, item, :SPECTRA] = result[:CHANS].astype(out_ref.dtype)
        out_ref[:, item, SPECTRA:] = result[CHANS:].astype(out_ref.dtype)


def channelize(voltages, keep):
    window = window_table()
    table = transform_table()
    count = voltages.shape[0]
    samples = voltages.reshape(count, SPECTRA + TAPS - 1, FRAME)
    order = jnp.arange(CHANS).reshape(-1, 2, 2).transpose(0, 2, 1).reshape(-1)
    table_t = jnp.transpose(table[:, :, order].reshape(FRAME, 2 * CHANS))
    group = 8
    return pl.pallas_call(
        transform_kernel,
        grid=(count // group,),
        in_specs=[
            pl.BlockSpec(memory_space=pltpu.SMEM),
            pl.BlockSpec((TAPS, FRAME), lambda g: (0, 0)),
            pl.BlockSpec((2 * CHANS, FRAME), lambda g: (0, 0)),
            pl.BlockSpec((group, SPECTRA + TAPS - 1, FRAME), lambda g: (g, 0, 0)),
        ],
        out_specs=pl.BlockSpec((CHANS, group, 2 * SPECTRA), lambda g: (0, g, 0)),
        out_shape=jax.ShapeDtypeStruct((CHANS, count, 2 * SPECTRA), jnp.bfloat16),
        scratch_shapes=[pltpu.VMEM((SPECTRA + 2 * TAPS, FRAME), jnp.float32)],
        cost_estimate=pl.CostEstimate(
            flops=2 * count * SPECTRA * FRAME * (2 * CHANS + TAPS),
            transcendentals=0,
            bytes_accessed=4 * count * (SPECTRA + TAPS) * FRAME + 2 * CHANS * count * 2 * SPECTRA,
        ),
    )(keep, window, table_t, samples)


def split3(value):
    high = value.astype(jnp.bfloat16)
    rest = value - high.astype(jnp.float32)
    mid = rest.astype(jnp.bfloat16)
    low = (rest - mid.astype(jnp.float32)).astype(jnp.bfloat16)
    return jnp.concatenate([high, mid, low], axis=-1)


def exact_dot(lhs, rhs_f32, dims):
    cols = rhs_f32.shape[-1]
    parts = lax.dot_general(
        lhs, split3(rhs_f32), (dims, ((), ())), preferred_element_type=jnp.float32
    )
    return parts[:, :cols] + parts[:, cols : 2 * cols] + parts[:, 2 * cols :]


def solve_gains(data, model_re, model_im):
    count = data.shape[0]

    def sweep(gain_re, gain_im):
        probe_re = gain_re * model_re - gain_im * model_im
        probe_im = gain_re * model_im + gain_im * model_re
        power = jnp.sum(probe_re * probe_re + probe_im * probe_im)
        half = exact_dot(data, jnp.stack([probe_re, probe_im], axis=1), ((0,), (0,)))
        u_re = half[:SPECTRA, 0] + half[SPECTRA:, 1]
        u_im = half[:SPECTRA, 1] - half[SPECTRA:, 0]
        mix = jnp.concatenate(
            [jnp.stack([u_re, u_im], axis=1), jnp.stack([-u_im, u_re], axis=1)], axis=0
        )
        product = exact_dot(data, mix, ((1,), (0,))) * (1.0 / SPECTRA)
        product_re = product[:, 0]
        product_im = product[:, 1]
        denominator = (model_re * model_re + model_im * model_im) * (power + 1e-06)
        new_re = (model_re * product_re + model_im * product_im) / denominator
        new_im = (model_re * product_im - model_im * product_re) / denominator
        return new_re, new_im

    def paired(step_index, carried):
        first_re, first_im = sweep(carried[0], carried[1])
        second_re, second_im = sweep(first_re, first_im)
        return (0.5 * (second_re + first_re), 0.5 * (second_im + first_im))

    start_re = jnp.ones((count,), jnp.float32)
    start_im = jnp.zeros((count,), jnp.float32)
    return lax.fori_loop(0, ITERS // 2, paired, (start_re, start_im), unroll=True)


def correlate_kernel(block_ref, rows_ref, cols_ref, out_ref, turned_ref):
    width = rows_ref.shape[-1]
    rows = rows_ref[:, 0].reshape(-1, width)

    @pl.when(pl.program_id(1) == 0)
    def _():
        turned_ref[:, :SPECTRA] = rows[:, SPECTRA:]
        turned_ref[:, SPECTRA:] = -rows[:, :SPECTRA]

    cols = cols_ref[:, 0].reshape(-1, width)
    dims = (((1,), (1,)), ((), ()))
    real = lax.dot_general(rows, cols, dims, preferred_element_type=jnp.float32)
    imag = lax.dot_general(turned_ref[...], cols, dims, preferred_element_type=jnp.float32)
    out_ref[0, 0] = (real * (1.0 / SPECTRA)).astype(out_ref.dtype)
    out_ref[1, 0] = (imag * (1.0 / SPECTRA)).astype(out_ref.dtype)


def correlate_into_kernel(block_ref, rows_ref, cols_ref, prev_ref, out_ref, turned_ref):
    correlate_kernel(block_ref, rows_ref, cols_ref, out_ref, turned_ref)


def correlate(data, scalars, row_count, out=None, total_chans=None, col_block=512):
    devices, chans, per, width = data.shape
    inputs = devices * per
    total_chans = chans if total_chans is None else total_chans
    grid = (chans, inputs // col_block)
    row_devices = row_count // per
    col_devices = col_block // per
    in_specs = [
        pl.BlockSpec((row_devices, 1, per, width), lambda c, j, s: (s[0], c, 0, 0)),
        pl.BlockSpec((col_devices, 1, per, width), lambda c, j, s: (j, c, 0, 0)),
    ]
    operands = [scalars, data, data]
    aliases = {}
    if out is not None:
        in_specs.append(pl.BlockSpec(memory_space=pl.ANY))
        operands.append(out)
        aliases = {3: 0}
    spec = pltpu.PrefetchScalarGridSpec(
        num_scalar_prefetch=1,
        grid=grid,
        in_specs=in_specs,
        out_specs=pl.BlockSpec((2, 1, row_count, col_block), lambda c, j, s: (0, s[1] + c, 0, j)),
        scratch_shapes=[pltpu.VMEM((row_count, width), data.dtype)],
    )
    flops = 8 * chans * row_count * inputs * (width // 2)
    kernel = correlate_kernel if out is None else correlate_into_kernel
    return pl.pallas_call(
        kernel,
        grid_spec=spec,
        out_shape=jax.ShapeDtypeStruct((2, total_chans, row_count, inputs), jnp.bfloat16),
        input_output_aliases=aliases,
        cost_estimate=pl.CostEstimate(
            flops=flops,
            transcendentals=0,
            bytes_accessed=2 * chans * (inputs * width + row_count * width + 2 * row_count * inputs),
        ),
    )(*operands)


def shards(voltages, flags, model_amp, model_phase):
    keep = (1 - flags).astype(jnp.float32)
    input_count = voltages.shape[0]
    spectra = channelize(voltages, keep)
    blk_count = lax.axis_size("blk")
    chan_count = lax.axis_size("chan")
    block_index = lax.axis_index("blk")
    spectra = spectra.reshape(chan_count, 2, 2, input_count, 2 * SPECTRA)
    first_send = spectra
    second_send = spectra[:, ::-1]
    devices = chan_count * blk_count

    def turn(send):
        send = send.reshape(devices, input_count, 2 * SPECTRA)
        return lax.all_to_all(send, ("chan", "blk"), split_axis=0, concat_axis=0, tiled=True)

    own = turn(first_send)
    all_inputs = devices * input_count
    row_count = all_inputs // blk_count
    core = block_index % 2
    level = block_index // 2
    swap = [(b, b ^ 1) for b in range(blk_count)]
    own_partner = lax.ppermute(own, "blk", perm=swap)

    solve = 2 * core + level
    amp = lax.dynamic_index_in_dim(model_amp, solve, 0, keepdims=False)
    phase = lax.dynamic_index_in_dim(model_phase, solve, 0, keepdims=False)
    full_re = amp * jnp.cos(phase)
    full_im = amp * jnp.sin(phase)
    other = turn(second_send)
    other_partner = lax.ppermute(other, "blk", perm=swap)
    solved = jnp.stack(solve_gains(own.reshape(all_inputs, -1), full_re, full_im))
    everyone = lax.all_gather(solved, ("chan", "blk"), axis=0, tiled=False)
    me = lax.axis_index("chan") * blk_count + block_index
    gains = lax.dynamic_slice_in_dim(everyone, me * input_count, input_count, 2)
    gains = gains.reshape(chan_count, 2, 2, 2, input_count)
    gains = jnp.transpose(gains, (3, 0, 2, 1, 4)).reshape(2, -1, input_count)

    local_chans = 4
    shape = (devices, 1, input_count, 2 * SPECTRA)
    visibility = None
    for data, chan in (
        (own, 2 * core + level),
        (other, 2 * core + 1 - level),
        (own_partner, 2 - 2 * core + level),
        (other_partner, 3 - 2 * core - level),
    ):
        scalars = jnp.stack([block_index, chan]).astype(jnp.int32)
        visibility = correlate(
            data.reshape(shape), scalars, row_count, out=visibility, total_chans=local_chans
        )
    return (visibility, gains)


def solution(mesh):
    return jax.shard_map(
        shards,
        mesh=mesh,
        in_specs=(P(("chan", "blk"), None), P(("chan", "blk")), P("chan", None), P("chan", None)),
        out_specs=(P(None, "chan", "blk", None), P(None, None, ("chan", "blk"))),
        check_vma=False,
    )
```

```python
import math

import jax
import jax.numpy as jnp
from jax import lax
from jax.experimental import pallas as pl
from jax.experimental.pallas import tpu as pltpu
from jax.sharding import PartitionSpec as P

CHANS = 128
FRAME = 512
TAPS = 8
BAND_START = 64
SPECTRA = 256
ITERS = 10


def window_table():
    index = jnp.arange(TAPS * FRAME, dtype=jnp.float32)
    offset = (index - TAPS * FRAME / 2 + 0.5) / FRAME
    taper = 0.5 - 0.5 * jnp.cos(2.0 * math.pi * (index + 0.5) / (TAPS * FRAME))
    return (jnp.sinc(offset) * taper).reshape(TAPS, FRAME)


def transform_table():
    sample = jnp.arange(FRAME, dtype=jnp.int32)
    channel = BAND_START + jnp.arange(CHANS, dtype=jnp.int32)
    angle = (sample[:, None] * channel[None, :] % FRAME).astype(jnp.float32) * (
        2.0 * math.pi / FRAME
    )
    return jnp.stack([jnp.cos(angle), -jnp.sin(angle)], axis=1).astype(jnp.bfloat16)


def transform_kernel(keep_ref, window_ref, table_ref, samples_ref, out_ref, wide_ref):
    group = samples_ref.shape[0]
    base = pl.program_id(0) * group
    scale = 1.0 / (64.0 * math.sqrt(FRAME))
    for item in range(group):
        wide_ref[0 : SPECTRA + TAPS - 1, :] = samples_ref[item].astype(jnp.float32)
        frames = window_ref[0:1, :] * wide_ref[0:SPECTRA, :]
        for tap in range(1, TAPS):
            frames = frames + window_ref[tap : tap + 1, :] * wide_ref[tap : tap + SPECTRA, :]
        result = lax.dot_general(
            table_ref[...], frames.astype(jnp.bfloat16), (((1,), (1,)), ((), ())),
            preferred_element_type=jnp.float32,
        )
        result = result * (scale * keep_ref[base + item])
        out_ref[:, item, :SPECTRA] = result[:CHANS].astype(out_ref.dtype)
        out_ref[:, item, SPECTRA:] = result[CHANS:].astype(out_ref.dtype)


def channelize(voltages, keep):
    window = window_table()
    table = transform_table()
    count = voltages.shape[0]
    samples = voltages.reshape(count, SPECTRA + TAPS - 1, FRAME)
    order = jnp.arange(CHANS).reshape(-1, 2, 2).transpose(0, 2, 1).reshape(-1)
    table_t = jnp.transpose(table[:, :, order].reshape(FRAME, 2 * CHANS))
    group = 8
    return pl.pallas_call(
        transform_kernel,
        grid=(count // group,),
        in_specs=[
            pl.BlockSpec(memory_space=pltpu.SMEM),
            pl.BlockSpec((TAPS, FRAME), lambda g: (0, 0)),
            pl.BlockSpec((2 * CHANS, FRAME), lambda g: (0, 0)),
            pl.BlockSpec((group, SPECTRA + TAPS - 1, FRAME), lambda g: (g, 0, 0)),
        ],
        out_specs=pl.BlockSpec((CHANS, group, 2 * SPECTRA), lambda g: (0, g, 0)),
        out_shape=jax.ShapeDtypeStruct((CHANS, count, 2 * SPECTRA), jnp.bfloat16),
        scratch_shapes=[pltpu.VMEM((SPECTRA + 2 * TAPS, FRAME), jnp.float32)],
        cost_estimate=pl.CostEstimate(
            flops=2 * count * SPECTRA * FRAME * (2 * CHANS + TAPS),
            transcendentals=0,
            bytes_accessed=4 * count * (SPECTRA + TAPS) * FRAME + 2 * CHANS * count * 2 * SPECTRA,
        ),
    )(keep, window, table_t, samples)


def split3(value):
    high = value.astype(jnp.bfloat16)
    rest = value - high.astype(jnp.float32)
    mid = rest.astype(jnp.bfloat16)
    low = (rest - mid.astype(jnp.float32)).astype(jnp.bfloat16)
    return jnp.concatenate([high, mid, low], axis=-1)


def exact_dot(lhs, rhs_f32, dims):
    cols = rhs_f32.shape[-1]
    parts = lax.dot_general(
        lhs, split3(rhs_f32), (dims, ((), ())), preferred_element_type=jnp.float32
    )
    return parts[:, :cols] + parts[:, cols : 2 * cols] + parts[:, 2 * cols :]


def solve_gains(data, model_re, model_im):
    count = data.shape[0]

    def sweep(gain_re, gain_im):
        probe_re = gain_re * model_re - gain_im * model_im
        probe_im = gain_re * model_im + gain_im * model_re
        power = jnp.sum(probe_re * probe_re + probe_im * probe_im)
        half = exact_dot(data, jnp.stack([probe_re, probe_im], axis=1), ((0,), (0,)))
        u_re = half[:SPECTRA, 0] + half[SPECTRA:, 1]
        u_im = half[:SPECTRA, 1] - half[SPECTRA:, 0]
        mix = jnp.concatenate(
            [jnp.stack([u_re, u_im], axis=1), jnp.stack([-u_im, u_re], axis=1)], axis=0
        )
        product = exact_dot(data, mix, ((1,), (0,))) * (1.0 / SPECTRA)
        product_re = product[:, 0]
        product_im = product[:, 1]
        denominator = (model_re * model_re + model_im * model_im) * (power + 1e-06)
        new_re = (model_re * product_re + model_im * product_im) / denominator
        new_im = (model_re * product_im - model_im * product_re) / denominator
        return new_re, new_im

    def paired(step_index, carried):
        first_re, first_im = sweep(carried[0], carried[1])
        second_re, second_im = sweep(first_re, first_im)
        return (0.5 * (second_re + first_re), 0.5 * (second_im + first_im))

    start_re = jnp.ones((count,), jnp.float32)
    start_im = jnp.zeros((count,), jnp.float32)
    return lax.fori_loop(0, ITERS // 2, paired, (start_re, start_im), unroll=True)


def correlate_kernel(block_ref, rows_ref, cols_ref, out_ref, turned_ref):
    width = rows_ref.shape[-1]
    rows = rows_ref[:, 0].reshape(-1, width)

    @pl.when(pl.program_id(1) == 0)
    def _():
        turned_ref[:, :SPECTRA] = rows[:, SPECTRA:]
        turned_ref[:, SPECTRA:] = -rows[:, :SPECTRA]

    cols = cols_ref[:, 0].reshape(-1, width)
    dims = (((1,), (1,)), ((), ()))
    real = lax.dot_general(rows, cols, dims, preferred_element_type=jnp.float32)
    imag = lax.dot_general(turned_ref[...], cols, dims, preferred_element_type=jnp.float32)
    out_ref[0, 0] = (real * (1.0 / SPECTRA)).astype(out_ref.dtype)
    out_ref[1, 0] = (imag * (1.0 / SPECTRA)).astype(out_ref.dtype)


def correlate_into_kernel(block_ref, rows_ref, cols_ref, prev_ref, out_ref, turned_ref):
    correlate_kernel(block_ref, rows_ref, cols_ref, out_ref, turned_ref)


def correlate(data, scalars, row_count, out=None, total_chans=None, col_block=512):
    devices, chans, per, width = data.shape
    inputs = devices * per
    total_chans = chans if total_chans is None else total_chans
    grid = (chans, inputs // col_block)
    row_devices = row_count // per
    col_devices = col_block // per
    in_specs = [
        pl.BlockSpec((row_devices, 1, per, width), lambda c, j, s: (s[0], c, 0, 0)),
        pl.BlockSpec((col_devices, 1, per, width), lambda c, j, s: (j, c, 0, 0)),
    ]
    operands = [scalars, data, data]
    aliases = {}
    if out is not None:
        in_specs.append(pl.BlockSpec(memory_space=pl.ANY))
        operands.append(out)
        aliases = {3: 0}
    spec = pltpu.PrefetchScalarGridSpec(
        num_scalar_prefetch=1,
        grid=grid,
        in_specs=in_specs,
        out_specs=pl.BlockSpec((2, 1, row_count, col_block), lambda c, j, s: (0, s[1] + c, 0, j)),
        scratch_shapes=[pltpu.VMEM((row_count, width), data.dtype)],
    )
    flops = 8 * chans * row_count * inputs * (width // 2)
    kernel = correlate_kernel if out is None else correlate_into_kernel
    return pl.pallas_call(
        kernel,
        grid_spec=spec,
        out_shape=jax.ShapeDtypeStruct((2, total_chans, row_count, inputs), jnp.bfloat16),
        input_output_aliases=aliases,
        cost_estimate=pl.CostEstimate(
            flops=flops,
            transcendentals=0,
            bytes_accessed=2 * chans * (inputs * width + row_count * width + 2 * row_count * inputs),
        ),
    )(*operands)


def shards(voltages, flags, model_amp, model_phase):
    keep = (1 - flags).astype(jnp.float32)
    input_count = voltages.shape[0]
    spectra = channelize(voltages, keep)
    blk_count = lax.axis_size("blk")
    chan_count = lax.axis_size("chan")
    block_index = lax.axis_index("blk")
    spectra = spectra.reshape(chan_count, 2, 2, input_count, 2 * SPECTRA)
    first_send = spectra
    second_send = spectra[:, ::-1]
    devices = chan_count * blk_count

    def turn(send):
        send = send.reshape(devices, input_count, 2 * SPECTRA)
        return lax.all_to_all(send, ("chan", "blk"), split_axis=0, concat_axis=0, tiled=True)

    own = turn(first_send)
    all_inputs = devices * input_count
    row_count = all_inputs // blk_count
    core = block_index % 2
    level = block_index // 2
    swap = [(b, b ^ 1) for b in range(blk_count)]
    own_partner = lax.ppermute(own, "blk", perm=swap)

    solve = 2 * core + level
    amp = lax.dynamic_index_in_dim(model_amp, solve, 0, keepdims=False)
    phase = lax.dynamic_index_in_dim(model_phase, solve, 0, keepdims=False)
    full_re = amp * jnp.cos(phase)
    full_im = amp * jnp.sin(phase)
    other = turn(second_send)
    other_partner = lax.ppermute(other, "blk", perm=swap)
    local_chans = 4
    shape = (devices, 1, input_count, 2 * SPECTRA)

    def correlate_into(visibility, data, chan):
        scalars = jnp.stack([block_index, chan]).astype(jnp.int32)
        return correlate(
            data.reshape(shape), scalars, row_count, out=visibility, total_chans=local_chans
        )

    visibility = correlate_into(None, own, 2 * core + level)
    own, visibility = lax.optimization_barrier((own, visibility))
    solved = jnp.stack(solve_gains(own.reshape(all_inputs, -1), full_re, full_im))
    owners = solved.reshape(2, devices, 1, input_count)
    gains = lax.all_to_all(owners, ("chan", "blk"), split_axis=1, concat_axis=1, tiled=True)
    gains = gains.reshape(2, chan_count, 2, 2, input_count)
    gains = jnp.swapaxes(gains, 2, 3).reshape(2, -1, input_count)

    for data, chan in (
        (other, 2 * core + 1 - level),
        (own_partner, 2 - 2 * core + level),
        (other_partner, 3 - 2 * core - level),
    ):
        visibility = correlate_into(visibility, data, chan)
    return (visibility, gains)


def solution(mesh):
    return jax.shard_map(
        shards,
        mesh=mesh,
        in_specs=(P(("chan", "blk"), None), P(("chan", "blk")), P("chan", None), P("chan", None)),
        out_specs=(P(None, "chan", "blk", None), P(None, None, ("chan", "blk"))),
        check_vma=False,
    )
```

```python
import math

import jax
import jax.numpy as jnp
from jax import lax
from jax.experimental import pallas as pl
from jax.experimental.pallas import tpu as pltpu
from jax.sharding import PartitionSpec as P

CHANS = 128
FRAME = 512
TAPS = 8
BAND_START = 64
SPECTRA = 256
ITERS = 10


def window_table():
    index = jnp.arange(TAPS * FRAME, dtype=jnp.float32)
    offset = (index - TAPS * FRAME / 2 + 0.5) / FRAME
    taper = 0.5 - 0.5 * jnp.cos(2.0 * math.pi * (index + 0.5) / (TAPS * FRAME))
    return (jnp.sinc(offset) * taper).reshape(TAPS, FRAME)


def transform_table():
    sample = jnp.arange(FRAME, dtype=jnp.int32)
    channel = BAND_START + jnp.arange(CHANS, dtype=jnp.int32)
    angle = (sample[:, None] * channel[None, :] % FRAME).astype(jnp.float32) * (
        2.0 * math.pi / FRAME
    )
    return jnp.stack([jnp.cos(angle), -jnp.sin(angle)], axis=1).astype(jnp.bfloat16)


def transform_kernel(keep_ref, window_ref, table_ref, samples_ref, out_ref, wide_ref):
    group = samples_ref.shape[0]
    base = pl.program_id(0) * group
    scale = 1.0 / (64.0 * math.sqrt(FRAME))
    for item in range(group):
        wide_ref[0 : SPECTRA + TAPS - 1, :] = samples_ref[item].astype(jnp.float32)
        frames = window_ref[0:1, :] * wide_ref[0:SPECTRA, :]
        for tap in range(1, TAPS):
            frames = frames + window_ref[tap : tap + 1, :] * wide_ref[tap : tap + SPECTRA, :]
        result = lax.dot_general(
            table_ref[...], frames.astype(jnp.bfloat16), (((1,), (1,)), ((), ())),
            preferred_element_type=jnp.float32,
        )
        result = result * (scale * keep_ref[base + item])
        out_ref[:, item, :SPECTRA] = result[:CHANS].astype(out_ref.dtype)
        out_ref[:, item, SPECTRA:] = result[CHANS:].astype(out_ref.dtype)


def channelize(voltages, keep):
    window = window_table()
    table = transform_table()
    count = voltages.shape[0]
    samples = voltages.reshape(count, SPECTRA + TAPS - 1, FRAME)
    order = jnp.arange(CHANS).reshape(-1, 2, 2).transpose(0, 2, 1).reshape(-1)
    table_t = jnp.transpose(table[:, :, order].reshape(FRAME, 2 * CHANS))
    group = 8
    return pl.pallas_call(
        transform_kernel,
        grid=(count // group,),
        in_specs=[
            pl.BlockSpec(memory_space=pltpu.SMEM),
            pl.BlockSpec((TAPS, FRAME), lambda g: (0, 0)),
            pl.BlockSpec((2 * CHANS, FRAME), lambda g: (0, 0)),
            pl.BlockSpec((group, SPECTRA + TAPS - 1, FRAME), lambda g: (g, 0, 0)),
        ],
        out_specs=pl.BlockSpec((CHANS, group, 2 * SPECTRA), lambda g: (0, g, 0)),
        out_shape=jax.ShapeDtypeStruct((CHANS, count, 2 * SPECTRA), jnp.bfloat16),
        scratch_shapes=[pltpu.VMEM((SPECTRA + 2 * TAPS, FRAME), jnp.float32)],
        cost_estimate=pl.CostEstimate(
            flops=2 * count * SPECTRA * FRAME * (2 * CHANS + TAPS),
            transcendentals=0,
            bytes_accessed=4 * count * (SPECTRA + TAPS) * FRAME + 2 * CHANS * count * 2 * SPECTRA,
        ),
    )(keep, window, table_t, samples)


def split3(value):
    high = value.astype(jnp.bfloat16)
    rest = value - high.astype(jnp.float32)
    mid = rest.astype(jnp.bfloat16)
    low = (rest - mid.astype(jnp.float32)).astype(jnp.bfloat16)
    return jnp.concatenate([high, mid, low], axis=-1)


def exact_dot(lhs, rhs_f32, dims):
    cols = rhs_f32.shape[-1]
    parts = lax.dot_general(
        lhs, split3(rhs_f32), (dims, ((), ())), preferred_element_type=jnp.float32
    )
    return parts[:, :cols] + parts[:, cols : 2 * cols] + parts[:, 2 * cols :]


def solve_gains(data, model_re, model_im):
    count = data.shape[0]

    def sweep(gain_re, gain_im):
        probe_re = gain_re * model_re - gain_im * model_im
        probe_im = gain_re * model_im + gain_im * model_re
        power = jnp.sum(probe_re * probe_re + probe_im * probe_im)
        half = exact_dot(data, jnp.stack([probe_re, probe_im], axis=1), ((0,), (0,)))
        u_re = half[:SPECTRA, 0] + half[SPECTRA:, 1]
        u_im = half[:SPECTRA, 1] - half[SPECTRA:, 0]
        mix = jnp.concatenate(
            [jnp.stack([u_re, u_im], axis=1), jnp.stack([-u_im, u_re], axis=1)], axis=0
        )
        product = exact_dot(data, mix, ((1,), (0,))) * (1.0 / SPECTRA)
        product_re = product[:, 0]
        product_im = product[:, 1]
        denominator = (model_re * model_re + model_im * model_im) * (power + 1e-06)
        new_re = (model_re * product_re + model_im * product_im) / denominator
        new_im = (model_re * product_im - model_im * product_re) / denominator
        return new_re, new_im

    def paired(step_index, carried):
        first_re, first_im = sweep(carried[0], carried[1])
        second_re, second_im = sweep(first_re, first_im)
        return (0.5 * (second_re + first_re), 0.5 * (second_im + first_im))

    start_re = jnp.ones((count,), jnp.float32)
    start_im = jnp.zeros((count,), jnp.float32)
    return lax.fori_loop(0, ITERS // 2, paired, (start_re, start_im), unroll=True)


def correlate_kernel(block_ref, rows_ref, cols_ref, out_ref, turned_ref):
    width = rows_ref.shape[-1]
    rows = rows_ref[:, 0].reshape(-1, width)

    @pl.when(pl.program_id(1) == 0)
    def _():
        turned_ref[:, :SPECTRA] = rows[:, SPECTRA:]
        turned_ref[:, SPECTRA:] = -rows[:, :SPECTRA]

    cols = cols_ref[:, 0].reshape(-1, width)
    dims = (((1,), (1,)), ((), ()))
    real = lax.dot_general(rows, cols, dims, preferred_element_type=jnp.float32)
    imag = lax.dot_general(turned_ref[...], cols, dims, preferred_element_type=jnp.float32)
    out_ref[0, 0] = (real * (1.0 / SPECTRA)).astype(out_ref.dtype)
    out_ref[1, 0] = (imag * (1.0 / SPECTRA)).astype(out_ref.dtype)


def correlate_into_kernel(block_ref, rows_ref, cols_ref, prev_ref, out_ref, turned_ref):
    correlate_kernel(block_ref, rows_ref, cols_ref, out_ref, turned_ref)


def correlate(data, scalars, row_count, out=None, total_chans=None, col_block=512):
    devices, chans, per, width = data.shape
    inputs = devices * per
    total_chans = chans if total_chans is None else total_chans
    grid = (chans, inputs // col_block)
    row_devices = row_count // per
    col_devices = col_block // per
    in_specs = [
        pl.BlockSpec((row_devices, 1, per, width), lambda c, j, s: (s[0], c, 0, 0)),
        pl.BlockSpec((col_devices, 1, per, width), lambda c, j, s: (j, c, 0, 0)),
    ]
    operands = [scalars, data, data]
    aliases = {}
    if out is not None:
        in_specs.append(pl.BlockSpec(memory_space=pl.ANY))
        operands.append(out)
        aliases = {3: 0}
    spec = pltpu.PrefetchScalarGridSpec(
        num_scalar_prefetch=1,
        grid=grid,
        in_specs=in_specs,
        out_specs=pl.BlockSpec((2, 1, row_count, col_block), lambda c, j, s: (0, s[1] + c, 0, j)),
        scratch_shapes=[pltpu.VMEM((row_count, width), data.dtype)],
    )
    flops = 8 * chans * row_count * inputs * (width // 2)
    kernel = correlate_kernel if out is None else correlate_into_kernel
    return pl.pallas_call(
        kernel,
        grid_spec=spec,
        out_shape=jax.ShapeDtypeStruct((2, total_chans, row_count, inputs), jnp.bfloat16),
        input_output_aliases=aliases,
        cost_estimate=pl.CostEstimate(
            flops=flops,
            transcendentals=0,
            bytes_accessed=2 * chans * (inputs * width + row_count * width + 2 * row_count * inputs),
        ),
    )(*operands)


def shards(voltages, flags, model_amp, model_phase):
    keep = (1 - flags).astype(jnp.float32)
    input_count = voltages.shape[0]
    spectra = channelize(voltages, keep)
    blk_count = lax.axis_size("blk")
    chan_count = lax.axis_size("chan")
    block_index = lax.axis_index("blk")
    spectra = spectra.reshape(chan_count, 2, 2, input_count, 2 * SPECTRA)
    first_send = spectra
    second_send = spectra[:, ::-1]
    devices = chan_count * blk_count

    def turn(send):
        send = send.reshape(devices, input_count, 2 * SPECTRA)
        return lax.all_to_all(send, ("chan", "blk"), split_axis=0, concat_axis=0, tiled=True)

    own = turn(first_send)
    all_inputs = devices * input_count
    row_count = all_inputs // blk_count
    core = block_index % 2
    level = block_index // 2
    swap = [(b, b ^ 1) for b in range(blk_count)]
    own_partner = lax.ppermute(own, "blk", perm=swap)

    solve = 2 * core + level
    amp = lax.dynamic_index_in_dim(model_amp, solve, 0, keepdims=False)
    phase = lax.dynamic_index_in_dim(model_phase, solve, 0, keepdims=False)
    full_re = amp * jnp.cos(phase)
    full_im = amp * jnp.sin(phase)
    other = turn(second_send)
    other_partner = lax.ppermute(other, "blk", perm=swap)
    local_chans = 4
    shape = (devices, 1, input_count, 2 * SPECTRA)

    def correlate_into(visibility, data, chan):
        scalars = jnp.stack([block_index, chan]).astype(jnp.int32)
        return correlate(
            data.reshape(shape), scalars, row_count, out=visibility, total_chans=local_chans
        )

    solved = jnp.stack(solve_gains(own.reshape(all_inputs, -1), full_re, full_im))
    owners = solved.reshape(2, devices, 1, input_count)
    gains = lax.all_to_all(owners, ("chan", "blk"), split_axis=1, concat_axis=1, tiled=True)
    gains = gains.reshape(2, chan_count, 2, 2, input_count)
    gains = jnp.swapaxes(gains, 2, 3).reshape(2, -1, input_count)

    visibility = None
    for data, chan in (
        (own, 2 * core + level),
        (other, 2 * core + 1 - level),
        (own_partner, 2 - 2 * core + level),
        (other_partner, 3 - 2 * core - level),
    ):
        visibility = correlate_into(visibility, data, chan)
    return (visibility, gains)


def solution(mesh):
    return jax.shard_map(
        shards,
        mesh=mesh,
        in_specs=(P(("chan", "blk"), None), P(("chan", "blk")), P("chan", None), P("chan", None)),
        out_specs=(P(None, "chan", "blk", None), P(None, None, ("chan", "blk"))),
        check_vma=False,
    )
```

```python
import math

import jax
import jax.numpy as jnp
from jax import lax
from jax.experimental import pallas as pl
from jax.experimental.pallas import tpu as pltpu
from jax.sharding import PartitionSpec as P

CHANS = 128
FRAME = 512
TAPS = 8
BAND_START = 64
SPECTRA = 256
ITERS = 10


def window_table():
    index = jnp.arange(TAPS * FRAME, dtype=jnp.float32)
    offset = (index - TAPS * FRAME / 2 + 0.5) / FRAME
    taper = 0.5 - 0.5 * jnp.cos(2.0 * math.pi * (index + 0.5) / (TAPS * FRAME))
    return (jnp.sinc(offset) * taper).reshape(TAPS, FRAME)


def transform_table():
    sample = jnp.arange(FRAME, dtype=jnp.int32)
    channel = BAND_START + jnp.arange(CHANS, dtype=jnp.int32)
    angle = (sample[:, None] * channel[None, :] % FRAME).astype(jnp.float32) * (
        2.0 * math.pi / FRAME
    )
    return jnp.stack([jnp.cos(angle), -jnp.sin(angle)], axis=1).astype(jnp.bfloat16)


def transform_kernel(keep_ref, window_ref, table_ref, samples_ref, out_ref, frames_ref):
    group = samples_ref.shape[1]
    base = pl.program_id(0) * group
    scale = 1.0 / (64.0 * math.sqrt(FRAME))

    def frame(step, carry):
        acc = window_ref[0:1, :] * samples_ref[step].astype(jnp.float32)
        for tap in range(1, TAPS):
            acc = acc + window_ref[tap : tap + 1, :] * samples_ref[step + tap].astype(jnp.float32)
        rows = pl.ds(pl.multiple_of(step * group, group), group)
        for lane in range(FRAME // 128):
            frames_ref[lane, rows, :] = acc[:, lane * 128 : (lane + 1) * 128]
        return carry

    lax.fori_loop(0, SPECTRA, frame, 0)
    for item in range(group):
        frames = jnp.concatenate(
            [frames_ref[lane, pl.ds(item, SPECTRA, stride=group), :] for lane in range(FRAME // 128)],
            axis=1,
        )
        result = lax.dot_general(
            table_ref[...], frames.astype(jnp.bfloat16), (((1,), (1,)), ((), ())),
            preferred_element_type=jnp.float32,
        )
        result = result * (scale * keep_ref[base + item])
        out_ref[:, item, :SPECTRA] = result[:CHANS].astype(out_ref.dtype)
        out_ref[:, item, SPECTRA:] = result[CHANS:].astype(out_ref.dtype)


def channelize(voltages, keep):
    window = window_table()
    table = transform_table()
    count = voltages.shape[0]
    samples = jnp.transpose(voltages.reshape(count, SPECTRA + TAPS - 1, FRAME), (1, 0, 2))
    order = jnp.arange(CHANS).reshape(-1, 2, 2).transpose(0, 2, 1).reshape(-1)
    table_t = jnp.transpose(table[:, :, order].reshape(FRAME, 2 * CHANS))
    group = 8
    return pl.pallas_call(
        transform_kernel,
        grid=(count // group,),
        in_specs=[
            pl.BlockSpec(memory_space=pltpu.SMEM),
            pl.BlockSpec((TAPS, FRAME), lambda g: (0, 0)),
            pl.BlockSpec((2 * CHANS, FRAME), lambda g: (0, 0)),
            pl.BlockSpec((SPECTRA + TAPS - 1, group, FRAME), lambda g: (0, g, 0)),
        ],
        out_specs=pl.BlockSpec((CHANS, group, 2 * SPECTRA), lambda g: (0, g, 0)),
        out_shape=jax.ShapeDtypeStruct((CHANS, count, 2 * SPECTRA), jnp.bfloat16),
        scratch_shapes=[pltpu.VMEM((FRAME // 128, SPECTRA * group, 128), jnp.float32)],
        cost_estimate=pl.CostEstimate(
            flops=2 * count * SPECTRA * FRAME * (2 * CHANS + TAPS),
            transcendentals=0,
            bytes_accessed=4 * count * (SPECTRA + TAPS) * FRAME + 2 * CHANS * count * 2 * SPECTRA,
        ),
    )(keep, window, table_t, samples)


def split3(value):
    high = value.astype(jnp.bfloat16)
    rest = value - high.astype(jnp.float32)
    mid = rest.astype(jnp.bfloat16)
    low = (rest - mid.astype(jnp.float32)).astype(jnp.bfloat16)
    return jnp.concatenate([high, mid, low], axis=-1)


def exact_dot(lhs, rhs_f32, dims):
    cols = rhs_f32.shape[-1]
    parts = lax.dot_general(
        lhs, split3(rhs_f32), (dims, ((), ())), preferred_element_type=jnp.float32
    )
    return parts[:, :cols] + parts[:, cols : 2 * cols] + parts[:, 2 * cols :]


def solve_gains(data, model_re, model_im):
    count = data.shape[0]

    def sweep(gain_re, gain_im):
        probe_re = gain_re * model_re - gain_im * model_im
        probe_im = gain_re * model_im + gain_im * model_re
        power = jnp.sum(probe_re * probe_re + probe_im * probe_im)
        half = exact_dot(data, jnp.stack([probe_re, probe_im], axis=1), ((0,), (0,)))
        u_re = half[:SPECTRA, 0] + half[SPECTRA:, 1]
        u_im = half[:SPECTRA, 1] - half[SPECTRA:, 0]
        mix = jnp.concatenate(
            [jnp.stack([u_re, u_im], axis=1), jnp.stack([-u_im, u_re], axis=1)], axis=0
        )
        product = exact_dot(data, mix, ((1,), (0,))) * (1.0 / SPECTRA)
        product_re = product[:, 0]
        product_im = product[:, 1]
        denominator = (model_re * model_re + model_im * model_im) * (power + 1e-06)
        new_re = (model_re * product_re + model_im * product_im) / denominator
        new_im = (model_re * product_im - model_im * product_re) / denominator
        return new_re, new_im

    def paired(step_index, carried):
        first_re, first_im = sweep(carried[0], carried[1])
        second_re, second_im = sweep(first_re, first_im)
        return (0.5 * (second_re + first_re), 0.5 * (second_im + first_im))

    start_re = jnp.ones((count,), jnp.float32)
    start_im = jnp.zeros((count,), jnp.float32)
    return lax.fori_loop(0, ITERS // 2, paired, (start_re, start_im), unroll=True)


def correlate_kernel(block_ref, rows_ref, cols_ref, out_ref, turned_ref):
    width = rows_ref.shape[-1]
    rows = rows_ref[:, 0].reshape(-1, width)

    @pl.when(pl.program_id(1) == 0)
    def _():
        turned_ref[:, :SPECTRA] = rows[:, SPECTRA:]
        turned_ref[:, SPECTRA:] = -rows[:, :SPECTRA]

    cols = cols_ref[:, 0].reshape(-1, width)
    dims = (((1,), (1,)), ((), ()))
    real = lax.dot_general(rows, cols, dims, preferred_element_type=jnp.float32)
    imag = lax.dot_general(turned_ref[...], cols, dims, preferred_element_type=jnp.float32)
    out_ref[0, 0] = (real * (1.0 / SPECTRA)).astype(out_ref.dtype)
    out_ref[1, 0] = (imag * (1.0 / SPECTRA)).astype(out_ref.dtype)


def correlate_into_kernel(block_ref, rows_ref, cols_ref, prev_ref, out_ref, turned_ref):
    correlate_kernel(block_ref, rows_ref, cols_ref, out_ref, turned_ref)


def correlate(data, scalars, row_count, out=None, total_chans=None, col_block=512):
    devices, chans, per, width = data.shape
    inputs = devices * per
    total_chans = chans if total_chans is None else total_chans
    grid = (chans, inputs // col_block)
    row_devices = row_count // per
    col_devices = col_block // per
    in_specs = [
        pl.BlockSpec((row_devices, 1, per, width), lambda c, j, s: (s[0], c, 0, 0)),
        pl.BlockSpec((col_devices, 1, per, width), lambda c, j, s: (j, c, 0, 0)),
    ]
    operands = [scalars, data, data]
    aliases = {}
    if out is not None:
        in_specs.append(pl.BlockSpec(memory_space=pl.ANY))
        operands.append(out)
        aliases = {3: 0}
    spec = pltpu.PrefetchScalarGridSpec(
        num_scalar_prefetch=1,
        grid=grid,
        in_specs=in_specs,
        out_specs=pl.BlockSpec((2, 1, row_count, col_block), lambda c, j, s: (0, s[1] + c, 0, j)),
        scratch_shapes=[pltpu.VMEM((row_count, width), data.dtype)],
    )
    flops = 8 * chans * row_count * inputs * (width // 2)
    kernel = correlate_kernel if out is None else correlate_into_kernel
    return pl.pallas_call(
        kernel,
        grid_spec=spec,
        out_shape=jax.ShapeDtypeStruct((2, total_chans, row_count, inputs), jnp.bfloat16),
        input_output_aliases=aliases,
        cost_estimate=pl.CostEstimate(
            flops=flops,
            transcendentals=0,
            bytes_accessed=2 * chans * (inputs * width + row_count * width + 2 * row_count * inputs),
        ),
    )(*operands)


def shards(voltages, flags, model_amp, model_phase):
    keep = (1 - flags).astype(jnp.float32)
    input_count = voltages.shape[0]
    spectra = channelize(voltages, keep)
    blk_count = lax.axis_size("blk")
    chan_count = lax.axis_size("chan")
    block_index = lax.axis_index("blk")
    spectra = spectra.reshape(chan_count, 2, 2, input_count, 2 * SPECTRA)
    first_send = spectra
    second_send = spectra[:, ::-1]
    devices = chan_count * blk_count

    def turn(send):
        send = send.reshape(devices, input_count, 2 * SPECTRA)
        return lax.all_to_all(send, ("chan", "blk"), split_axis=0, concat_axis=0, tiled=True)

    own = turn(first_send)
    all_inputs = devices * input_count
    row_count = all_inputs // blk_count
    core = block_index % 2
    level = block_index // 2
    swap = [(b, b ^ 1) for b in range(blk_count)]
    own_partner = lax.ppermute(own, "blk", perm=swap)

    solve = 2 * core + level
    amp = lax.dynamic_index_in_dim(model_amp, solve, 0, keepdims=False)
    phase = lax.dynamic_index_in_dim(model_phase, solve, 0, keepdims=False)
    full_re = amp * jnp.cos(phase)
    full_im = amp * jnp.sin(phase)
    other = turn(second_send)
    other_partner = lax.ppermute(other, "blk", perm=swap)
    local_chans = 4
    shape = (devices, 1, input_count, 2 * SPECTRA)

    def correlate_into(visibility, data, chan):
        scalars = jnp.stack([block_index, chan]).astype(jnp.int32)
        return correlate(
            data.reshape(shape), scalars, row_count, out=visibility, total_chans=local_chans
        )

    solved = jnp.stack(solve_gains(own.reshape(all_inputs, -1), full_re, full_im))
    owners = solved.reshape(2, devices, 1, input_count)
    gains = lax.all_to_all(owners, ("chan", "blk"), split_axis=1, concat_axis=1, tiled=True)
    gains = gains.reshape(2, chan_count, 2, 2, input_count)
    gains = jnp.swapaxes(gains, 2, 3).reshape(2, -1, input_count)

    visibility = None
    for data, chan in (
        (own, 2 * core + level),
        (other, 2 * core + 1 - level),
        (own_partner, 2 - 2 * core + level),
        (other_partner, 3 - 2 * core - level),
    ):
        visibility = correlate_into(visibility, data, chan)
    return (visibility, gains)


def solution(mesh):
    return jax.shard_map(
        shards,
        mesh=mesh,
        in_specs=(P(("chan", "blk"), None), P(("chan", "blk")), P("chan", None), P("chan", None)),
        out_specs=(P(None, "chan", "blk", None), P(None, None, ("chan", "blk"))),
        check_vma=False,
    )
```

```python
import math

import jax
import jax.numpy as jnp
from jax import lax
from jax.experimental import pallas as pl
from jax.experimental.pallas import tpu as pltpu
from jax.sharding import PartitionSpec as P

CHANS = 128
FRAME = 512
TAPS = 8
BAND_START = 64
SPECTRA = 256
ITERS = 10


def window_table():
    index = jnp.arange(TAPS * FRAME, dtype=jnp.float32)
    offset = (index - TAPS * FRAME / 2 + 0.5) / FRAME
    taper = 0.5 - 0.5 * jnp.cos(2.0 * math.pi * (index + 0.5) / (TAPS * FRAME))
    return (jnp.sinc(offset) * taper).reshape(TAPS, FRAME)


def transform_table():
    sample = jnp.arange(FRAME, dtype=jnp.int32)
    channel = BAND_START + jnp.arange(CHANS, dtype=jnp.int32)
    angle = (sample[:, None] * channel[None, :] % FRAME).astype(jnp.float32) * (
        2.0 * math.pi / FRAME
    )
    return jnp.stack([jnp.cos(angle), -jnp.sin(angle)], axis=1).astype(jnp.bfloat16)


def transform_kernel(keep_ref, window_ref, table_ref, samples_ref, out_ref, wide_ref):
    group = samples_ref.shape[0]
    base = pl.program_id(0) * group
    scale = 1.0 / (64.0 * math.sqrt(FRAME))
    for item in range(group):
        wide_ref[0 : SPECTRA + TAPS - 1, :] = samples_ref[item].astype(jnp.float32)
        frames = window_ref[0:1, :] * wide_ref[0:SPECTRA, :]
        for tap in range(1, TAPS):
            frames = frames + window_ref[tap : tap + 1, :] * wide_ref[tap : tap + SPECTRA, :]
        result = lax.dot_general(
            table_ref[...], frames.astype(jnp.bfloat16), (((1,), (1,)), ((), ())),
            preferred_element_type=jnp.float32,
        )
        result = result * (scale * keep_ref[base + item])
        out_ref[:, item, :SPECTRA] = result[:CHANS].astype(out_ref.dtype)
        out_ref[:, item, SPECTRA:] = result[CHANS:].astype(out_ref.dtype)


def channelize(voltages, keep):
    window = window_table()
    table = transform_table()
    count = voltages.shape[0]
    samples = voltages.reshape(count, SPECTRA + TAPS - 1, FRAME)
    order = jnp.arange(CHANS).reshape(-1, 2, 2).transpose(0, 2, 1).reshape(-1)
    table_t = jnp.transpose(table[:, :, order].reshape(FRAME, 2 * CHANS))
    group = 8
    return pl.pallas_call(
        transform_kernel,
        grid=(count // group,),
        in_specs=[
            pl.BlockSpec(memory_space=pltpu.SMEM),
            pl.BlockSpec((TAPS, FRAME), lambda g: (0, 0)),
            pl.BlockSpec((2 * CHANS, FRAME), lambda g: (0, 0)),
            pl.BlockSpec((group, SPECTRA + TAPS - 1, FRAME), lambda g: (g, 0, 0)),
        ],
        out_specs=pl.BlockSpec((CHANS, group, 2 * SPECTRA), lambda g: (0, g, 0)),
        out_shape=jax.ShapeDtypeStruct((CHANS, count, 2 * SPECTRA), jnp.bfloat16),
        scratch_shapes=[pltpu.VMEM((SPECTRA + 2 * TAPS, FRAME), jnp.float32)],
        cost_estimate=pl.CostEstimate(
            flops=2 * count * SPECTRA * FRAME * (2 * CHANS + TAPS),
            transcendentals=0,
            bytes_accessed=4 * count * (SPECTRA + TAPS) * FRAME + 2 * CHANS * count * 2 * SPECTRA,
        ),
    )(keep, window, table_t, samples)


def split3(value):
    high = value.astype(jnp.bfloat16)
    rest = value - high.astype(jnp.float32)
    mid = rest.astype(jnp.bfloat16)
    low = (rest - mid.astype(jnp.float32)).astype(jnp.bfloat16)
    return jnp.concatenate([high, mid, low], axis=-1)


def exact_dot(lhs, rhs_f32, dims):
    cols = rhs_f32.shape[-1]
    parts = lax.dot_general(
        lhs, split3(rhs_f32), (dims, ((), ())), preferred_element_type=jnp.float32
    )
    return parts[:, :cols] + parts[:, cols : 2 * cols] + parts[:, 2 * cols :]


def solve_gains(data, model_re, model_im):
    count = data.shape[0]

    def sweep(gain_re, gain_im):
        probe_re = gain_re * model_re - gain_im * model_im
        probe_im = gain_re * model_im + gain_im * model_re
        power = jnp.sum(probe_re * probe_re + probe_im * probe_im)
        half = exact_dot(data, jnp.stack([probe_re, probe_im], axis=1), ((0,), (0,)))
        u_re = half[:SPECTRA, 0] + half[SPECTRA:, 1]
        u_im = half[:SPECTRA, 1] - half[SPECTRA:, 0]
        mix = jnp.concatenate(
            [jnp.stack([u_re, u_im], axis=1), jnp.stack([-u_im, u_re], axis=1)], axis=0
        )
        product = exact_dot(data, mix, ((1,), (0,))) * (1.0 / SPECTRA)
        product_re = product[:, 0]
        product_im = product[:, 1]
        denominator = (model_re * model_re + model_im * model_im) * (power + 1e-06)
        new_re = (model_re * product_re + model_im * product_im) / denominator
        new_im = (model_re * product_im - model_im * product_re) / denominator
        return new_re, new_im

    def paired(step_index, carried):
        first_re, first_im = sweep(carried[0], carried[1])
        second_re, second_im = sweep(first_re, first_im)
        return (0.5 * (second_re + first_re), 0.5 * (second_im + first_im))

    start_re = jnp.ones((count,), jnp.float32)
    start_im = jnp.zeros((count,), jnp.float32)
    return lax.fori_loop(0, ITERS // 2, paired, (start_re, start_im), unroll=True)


def correlate_kernel(block_ref, rows_ref, cols_ref, out_ref, turned_ref):
    width = rows_ref.shape[-1]
    rows = rows_ref[:, 0].reshape(-1, width)

    @pl.when(pl.program_id(1) == 0)
    def _():
        turned_ref[:, :SPECTRA] = rows[:, SPECTRA:]
        turned_ref[:, SPECTRA:] = -rows[:, :SPECTRA]

    cols = cols_ref[:, 0].reshape(-1, width)
    dims = (((1,), (1,)), ((), ()))
    real = lax.dot_general(rows, cols, dims, preferred_element_type=jnp.float32)
    imag = lax.dot_general(turned_ref[...], cols, dims, preferred_element_type=jnp.float32)
    out_ref[0, 0] = (real * (1.0 / SPECTRA)).astype(out_ref.dtype)
    out_ref[1, 0] = (imag * (1.0 / SPECTRA)).astype(out_ref.dtype)


def correlate_into_kernel(block_ref, rows_ref, cols_ref, prev_ref, out_ref, turned_ref):
    correlate_kernel(block_ref, rows_ref, cols_ref, out_ref, turned_ref)


def correlate(data, scalars, row_count, out=None, total_chans=None, col_block=1024):
    devices, chans, per, width = data.shape
    inputs = devices * per
    total_chans = chans if total_chans is None else total_chans
    grid = (chans, inputs // col_block)
    row_devices = row_count // per
    col_devices = col_block // per
    in_specs = [
        pl.BlockSpec((row_devices, 1, per, width), lambda c, j, s: (s[0], c, 0, 0)),
        pl.BlockSpec((col_devices, 1, per, width), lambda c, j, s: (j, c, 0, 0)),
    ]
    operands = [scalars, data, data]
    aliases = {}
    if out is not None:
        in_specs.append(pl.BlockSpec(memory_space=pl.ANY))
        operands.append(out)
        aliases = {3: 0}
    spec = pltpu.PrefetchScalarGridSpec(
        num_scalar_prefetch=1,
        grid=grid,
        in_specs=in_specs,
        out_specs=pl.BlockSpec((2, 1, row_count, col_block), lambda c, j, s: (0, s[1] + c, 0, j)),
        scratch_shapes=[pltpu.VMEM((row_count, width), data.dtype)],
    )
    flops = 8 * chans * row_count * inputs * (width // 2)
    kernel = correlate_kernel if out is None else correlate_into_kernel
    return pl.pallas_call(
        kernel,
        grid_spec=spec,
        out_shape=jax.ShapeDtypeStruct((2, total_chans, row_count, inputs), jnp.bfloat16),
        input_output_aliases=aliases,
        cost_estimate=pl.CostEstimate(
            flops=flops,
            transcendentals=0,
            bytes_accessed=2 * chans * (inputs * width + row_count * width + 2 * row_count * inputs),
        ),
    )(*operands)


def shards(voltages, flags, model_amp, model_phase):
    keep = (1 - flags).astype(jnp.float32)
    input_count = voltages.shape[0]
    spectra = channelize(voltages, keep)
    blk_count = lax.axis_size("blk")
    chan_count = lax.axis_size("chan")
    block_index = lax.axis_index("blk")
    spectra = spectra.reshape(chan_count, 2, 2, input_count, 2 * SPECTRA)
    first_send = spectra
    second_send = spectra[:, ::-1]
    devices = chan_count * blk_count

    def turn(send):
        send = send.reshape(devices, input_count, 2 * SPECTRA)
        return lax.all_to_all(send, ("chan", "blk"), split_axis=0, concat_axis=0, tiled=True)

    own = turn(first_send)
    all_inputs = devices * input_count
    row_count = all_inputs // blk_count
    core = block_index % 2
    level = block_index // 2
    swap = [(b, b ^ 1) for b in range(blk_count)]
    own_partner = lax.ppermute(own, "blk", perm=swap)

    solve = 2 * core + level
    amp = lax.dynamic_index_in_dim(model_amp, solve, 0, keepdims=False)
    phase = lax.dynamic_index_in_dim(model_phase, solve, 0, keepdims=False)
    full_re = amp * jnp.cos(phase)
    full_im = amp * jnp.sin(phase)
    other = turn(second_send)
    other_partner = lax.ppermute(other, "blk", perm=swap)
    local_chans = 4
    shape = (devices, 1, input_count, 2 * SPECTRA)

    def correlate_into(visibility, data, chan):
        scalars = jnp.stack([block_index, chan]).astype(jnp.int32)
        return correlate(
            data.reshape(shape), scalars, row_count, out=visibility, total_chans=local_chans
        )

    solved = jnp.stack(solve_gains(own.reshape(all_inputs, -1), full_re, full_im))
    owners = solved.reshape(2, devices, 1, input_count)
    gains = lax.all_to_all(owners, ("chan", "blk"), split_axis=1, concat_axis=1, tiled=True)
    gains = gains.reshape(2, chan_count, 2, 2, input_count)
    gains = jnp.swapaxes(gains, 2, 3).reshape(2, -1, input_count)

    visibility = None
    for data, chan in (
        (own, 2 * core + level),
        (other, 2 * core + 1 - level),
        (own_partner, 2 - 2 * core + level),
        (other_partner, 3 - 2 * core - level),
    ):
        visibility = correlate_into(visibility, data, chan)
    return (visibility, gains)


def solution(mesh):
    return jax.shard_map(
        shards,
        mesh=mesh,
        in_specs=(P(("chan", "blk"), None), P(("chan", "blk")), P("chan", None), P("chan", None)),
        out_specs=(P(None, "chan", "blk", None), P(None, None, ("chan", "blk"))),
        check_vma=False,
    )
```

```python
import math

import jax
import jax.numpy as jnp
from jax import lax
from jax.experimental import pallas as pl
from jax.experimental.pallas import tpu as pltpu
from jax.sharding import PartitionSpec as P

CHANS = 128
FRAME = 512
TAPS = 8
BAND_START = 64
SPECTRA = 256
ITERS = 10


def window_table():
    index = jnp.arange(TAPS * FRAME, dtype=jnp.float32)
    offset = (index - TAPS * FRAME / 2 + 0.5) / FRAME
    taper = 0.5 - 0.5 * jnp.cos(2.0 * math.pi * (index + 0.5) / (TAPS * FRAME))
    return (jnp.sinc(offset) * taper).reshape(TAPS, FRAME)


def transform_table():
    sample = jnp.arange(FRAME, dtype=jnp.int32)
    channel = BAND_START + jnp.arange(CHANS, dtype=jnp.int32)
    angle = (sample[:, None] * channel[None, :] % FRAME).astype(jnp.float32) * (
        2.0 * math.pi / FRAME
    )
    return jnp.stack([jnp.cos(angle), -jnp.sin(angle)], axis=1).astype(jnp.bfloat16)


def transform_kernel(keep_ref, window_ref, table_ref, samples_ref, out_ref, wide_ref):
    group = samples_ref.shape[0]
    base = pl.program_id(0) * group
    scale = 1.0 / (64.0 * math.sqrt(FRAME))
    for item in range(group):
        wide_ref[0 : SPECTRA + TAPS - 1, :] = samples_ref[item].astype(jnp.float32)
        frames = window_ref[0:1, :] * wide_ref[0:SPECTRA, :]
        for tap in range(1, TAPS):
            frames = frames + window_ref[tap : tap + 1, :] * wide_ref[tap : tap + SPECTRA, :]
        result = lax.dot_general(
            table_ref[...], frames.astype(jnp.bfloat16), (((1,), (1,)), ((), ())),
            preferred_element_type=jnp.float32,
        )
        result = result * (scale * keep_ref[base + item])
        out_ref[:, item, :SPECTRA] = result[:CHANS].astype(out_ref.dtype)
        out_ref[:, item, SPECTRA:] = result[CHANS:].astype(out_ref.dtype)


def channelize(voltages, keep):
    window = window_table()
    table = transform_table()
    count = voltages.shape[0]
    samples = voltages.reshape(count, SPECTRA + TAPS - 1, FRAME)
    order = jnp.arange(CHANS).reshape(-1, 2, 2).transpose(0, 2, 1).reshape(-1)
    table_t = jnp.transpose(table[:, :, order].reshape(FRAME, 2 * CHANS))
    group = 8
    return pl.pallas_call(
        transform_kernel,
        grid=(count // group,),
        in_specs=[
            pl.BlockSpec(memory_space=pltpu.SMEM),
            pl.BlockSpec((TAPS, FRAME), lambda g: (0, 0)),
            pl.BlockSpec((2 * CHANS, FRAME), lambda g: (0, 0)),
            pl.BlockSpec((group, SPECTRA + TAPS - 1, FRAME), lambda g: (g, 0, 0)),
        ],
        out_specs=pl.BlockSpec((CHANS, group, 2 * SPECTRA), lambda g: (0, g, 0)),
        out_shape=jax.ShapeDtypeStruct((CHANS, count, 2 * SPECTRA), jnp.bfloat16),
        scratch_shapes=[pltpu.VMEM((SPECTRA + 2 * TAPS, FRAME), jnp.float32)],
        cost_estimate=pl.CostEstimate(
            flops=2 * count * SPECTRA * FRAME * (2 * CHANS + TAPS),
            transcendentals=0,
            bytes_accessed=4 * count * (SPECTRA + TAPS) * FRAME + 2 * CHANS * count * 2 * SPECTRA,
        ),
    )(keep, window, table_t, samples)


def split3(value):
    high = value.astype(jnp.bfloat16)
    rest = value - high.astype(jnp.float32)
    mid = rest.astype(jnp.bfloat16)
    low = (rest - mid.astype(jnp.float32)).astype(jnp.bfloat16)
    return jnp.concatenate([high, mid, low], axis=-1)


def exact_dot(lhs, rhs_f32, dims):
    cols = rhs_f32.shape[-1]
    parts = lax.dot_general(
        lhs, split3(rhs_f32), (dims, ((), ())), preferred_element_type=jnp.float32
    )
    return parts[:, :cols] + parts[:, cols : 2 * cols] + parts[:, 2 * cols :]


def solve_gains(data, model_re, model_im):
    count = data.shape[0]

    def sweep(gain_re, gain_im):
        probe_re = gain_re * model_re - gain_im * model_im
        probe_im = gain_re * model_im + gain_im * model_re
        power = jnp.sum(probe_re * probe_re + probe_im * probe_im)
        half = exact_dot(data, jnp.stack([probe_re, probe_im], axis=1), ((0,), (0,)))
        u_re = half[:SPECTRA, 0] + half[SPECTRA:, 1]
        u_im = half[:SPECTRA, 1] - half[SPECTRA:, 0]
        mix = jnp.concatenate(
            [jnp.stack([u_re, u_im], axis=1), jnp.stack([-u_im, u_re], axis=1)], axis=0
        )
        product = exact_dot(data, mix, ((1,), (0,))) * (1.0 / SPECTRA)
        product_re = product[:, 0]
        product_im = product[:, 1]
        denominator = (model_re * model_re + model_im * model_im) * (power + 1e-06)
        new_re = (model_re * product_re + model_im * product_im) / denominator
        new_im = (model_re * product_im - model_im * product_re) / denominator
        return new_re, new_im

    def paired(step_index, carried):
        first_re, first_im = sweep(carried[0], carried[1])
        second_re, second_im = sweep(first_re, first_im)
        return (0.5 * (second_re + first_re), 0.5 * (second_im + first_im))

    start_re = jnp.ones((count,), jnp.float32)
    start_im = jnp.zeros((count,), jnp.float32)
    return lax.fori_loop(0, ITERS // 2, paired, (start_re, start_im), unroll=True)


def correlate_kernel(block_ref, rows_ref, cols_ref, out_ref, turned_ref):
    width = rows_ref.shape[-1]
    rows = rows_ref[:, 0].reshape(-1, width)

    @pl.when(pl.program_id(1) == 0)
    def _():
        turned_ref[:, :SPECTRA] = rows[:, SPECTRA:]
        turned_ref[:, SPECTRA:] = -rows[:, :SPECTRA]

    cols = cols_ref[:, 0].reshape(-1, width)
    dims = (((1,), (1,)), ((), ()))
    real = lax.dot_general(rows, cols, dims, preferred_element_type=jnp.float32)
    imag = lax.dot_general(turned_ref[...], cols, dims, preferred_element_type=jnp.float32)
    out_ref[0, 0] = (real * (1.0 / SPECTRA)).astype(out_ref.dtype)
    out_ref[1, 0] = (imag * (1.0 / SPECTRA)).astype(out_ref.dtype)


def correlate_into_kernel(block_ref, rows_ref, cols_ref, prev_ref, out_ref, turned_ref):
    correlate_kernel(block_ref, rows_ref, cols_ref, out_ref, turned_ref)


def correlate(data, scalars, row_count, out=None, total_chans=None, col_block=2048):
    devices, chans, per, width = data.shape
    inputs = devices * per
    total_chans = chans if total_chans is None else total_chans
    grid = (chans, inputs // col_block)
    row_devices = row_count // per
    col_devices = col_block // per
    in_specs = [
        pl.BlockSpec((row_devices, 1, per, width), lambda c, j, s: (s[0], c, 0, 0)),
        pl.BlockSpec((col_devices, 1, per, width), lambda c, j, s: (j, c, 0, 0)),
    ]
    operands = [scalars, data, data]
    aliases = {}
    if out is not None:
        in_specs.append(pl.BlockSpec(memory_space=pl.ANY))
        operands.append(out)
        aliases = {3: 0}
    spec = pltpu.PrefetchScalarGridSpec(
        num_scalar_prefetch=1,
        grid=grid,
        in_specs=in_specs,
        out_specs=pl.BlockSpec((2, 1, row_count, col_block), lambda c, j, s: (0, s[1] + c, 0, j)),
        scratch_shapes=[pltpu.VMEM((row_count, width), data.dtype)],
    )
    flops = 8 * chans * row_count * inputs * (width // 2)
    kernel = correlate_kernel if out is None else correlate_into_kernel
    return pl.pallas_call(
        kernel,
        grid_spec=spec,
        out_shape=jax.ShapeDtypeStruct((2, total_chans, row_count, inputs), jnp.bfloat16),
        input_output_aliases=aliases,
        cost_estimate=pl.CostEstimate(
            flops=flops,
            transcendentals=0,
            bytes_accessed=2 * chans * (inputs * width + row_count * width + 2 * row_count * inputs),
        ),
    )(*operands)


def shards(voltages, flags, model_amp, model_phase):
    keep = (1 - flags).astype(jnp.float32)
    input_count = voltages.shape[0]
    spectra = channelize(voltages, keep)
    blk_count = lax.axis_size("blk")
    chan_count = lax.axis_size("chan")
    block_index = lax.axis_index("blk")
    spectra = spectra.reshape(chan_count, 2, 2, input_count, 2 * SPECTRA)
    first_send = spectra
    second_send = spectra[:, ::-1]
    devices = chan_count * blk_count

    def turn(send):
        send = send.reshape(devices, input_count, 2 * SPECTRA)
        return lax.all_to_all(send, ("chan", "blk"), split_axis=0, concat_axis=0, tiled=True)

    own = turn(first_send)
    all_inputs = devices * input_count
    row_count = all_inputs // blk_count
    core = block_index % 2
    level = block_index // 2
    swap = [(b, b ^ 1) for b in range(blk_count)]
    own_partner = lax.ppermute(own, "blk", perm=swap)

    solve = 2 * core + level
    amp = lax.dynamic_index_in_dim(model_amp, solve, 0, keepdims=False)
    phase = lax.dynamic_index_in_dim(model_phase, solve, 0, keepdims=False)
    full_re = amp * jnp.cos(phase)
    full_im = amp * jnp.sin(phase)
    other = turn(second_send)
    other_partner = lax.ppermute(other, "blk", perm=swap)
    local_chans = 4
    shape = (devices, 1, input_count, 2 * SPECTRA)

    def correlate_into(visibility, data, chan):
        scalars = jnp.stack([block_index, chan]).astype(jnp.int32)
        return correlate(
            data.reshape(shape), scalars, row_count, out=visibility, total_chans=local_chans
        )

    solved = jnp.stack(solve_gains(own.reshape(all_inputs, -1), full_re, full_im))
    owners = solved.reshape(2, devices, 1, input_count)
    gains = lax.all_to_all(owners, ("chan", "blk"), split_axis=1, concat_axis=1, tiled=True)
    gains = gains.reshape(2, chan_count, 2, 2, input_count)
    gains = jnp.swapaxes(gains, 2, 3).reshape(2, -1, input_count)

    visibility = None
    for data, chan in (
        (own, 2 * core + level),
        (other, 2 * core + 1 - level),
        (own_partner, 2 - 2 * core + level),
        (other_partner, 3 - 2 * core - level),
    ):
        visibility = correlate_into(visibility, data, chan)
    return (visibility, gains)


def solution(mesh):
    return jax.shard_map(
        shards,
        mesh=mesh,
        in_specs=(P(("chan", "blk"), None), P(("chan", "blk")), P("chan", None), P("chan", None)),
        out_specs=(P(None, "chan", "blk", None), P(None, None, ("chan", "blk"))),
        check_vma=False,
    )
```

```python
import math

import jax
import jax.numpy as jnp
from jax import lax
from jax.experimental import pallas as pl
from jax.experimental.pallas import tpu as pltpu
from jax.sharding import PartitionSpec as P

CHANS = 128
FRAME = 512
TAPS = 8
BAND_START = 64
SPECTRA = 256
ITERS = 10


def window_table():
    index = jnp.arange(TAPS * FRAME, dtype=jnp.float32)
    offset = (index - TAPS * FRAME / 2 + 0.5) / FRAME
    taper = 0.5 - 0.5 * jnp.cos(2.0 * math.pi * (index + 0.5) / (TAPS * FRAME))
    return (jnp.sinc(offset) * taper).reshape(TAPS, FRAME)


def transform_table():
    sample = jnp.arange(FRAME, dtype=jnp.int32)
    channel = BAND_START + jnp.arange(CHANS, dtype=jnp.int32)
    angle = (sample[:, None] * channel[None, :] % FRAME).astype(jnp.float32) * (
        2.0 * math.pi / FRAME
    )
    return jnp.stack([jnp.cos(angle), -jnp.sin(angle)], axis=1).astype(jnp.bfloat16)


def transform_kernel(keep_ref, window_ref, table_ref, samples_ref, out_ref, wide_ref):
    group = samples_ref.shape[0]
    base = pl.program_id(0) * group
    scale = 1.0 / (64.0 * math.sqrt(FRAME))
    for item in range(group):
        frames = window_ref[0:1, :] * samples_ref[item, 0:SPECTRA, :].astype(jnp.float32)
        for tap in range(1, TAPS):
            frames = frames + window_ref[tap : tap + 1, :] * samples_ref[
                item, tap : tap + SPECTRA, :
            ].astype(jnp.float32)
        result = lax.dot_general(
            table_ref[...], frames.astype(jnp.bfloat16), (((1,), (1,)), ((), ())),
            preferred_element_type=jnp.float32,
        )
        result = result * (scale * keep_ref[base + item])
        out_ref[:, item, :SPECTRA] = result[:CHANS].astype(out_ref.dtype)
        out_ref[:, item, SPECTRA:] = result[CHANS:].astype(out_ref.dtype)


def channelize(voltages, keep):
    window = window_table()
    table = transform_table()
    count = voltages.shape[0]
    samples = voltages.reshape(count, SPECTRA + TAPS - 1, FRAME)
    order = jnp.arange(CHANS).reshape(-1, 2, 2).transpose(0, 2, 1).reshape(-1)
    table_t = jnp.transpose(table[:, :, order].reshape(FRAME, 2 * CHANS))
    group = 8
    return pl.pallas_call(
        transform_kernel,
        grid=(count // group,),
        in_specs=[
            pl.BlockSpec(memory_space=pltpu.SMEM),
            pl.BlockSpec((TAPS, FRAME), lambda g: (0, 0)),
            pl.BlockSpec((2 * CHANS, FRAME), lambda g: (0, 0)),
            pl.BlockSpec((group, SPECTRA + TAPS - 1, FRAME), lambda g: (g, 0, 0)),
        ],
        out_specs=pl.BlockSpec((CHANS, group, 2 * SPECTRA), lambda g: (0, g, 0)),
        out_shape=jax.ShapeDtypeStruct((CHANS, count, 2 * SPECTRA), jnp.bfloat16),
        scratch_shapes=[pltpu.VMEM((SPECTRA + 2 * TAPS, FRAME), jnp.float32)],
        cost_estimate=pl.CostEstimate(
            flops=2 * count * SPECTRA * FRAME * (2 * CHANS + TAPS),
            transcendentals=0,
            bytes_accessed=4 * count * (SPECTRA + TAPS) * FRAME + 2 * CHANS * count * 2 * SPECTRA,
        ),
    )(keep, window, table_t, samples)


def split3(value):
    high = value.astype(jnp.bfloat16)
    rest = value - high.astype(jnp.float32)
    mid = rest.astype(jnp.bfloat16)
    low = (rest - mid.astype(jnp.float32)).astype(jnp.bfloat16)
    return jnp.concatenate([high, mid, low], axis=-1)


def exact_dot(lhs, rhs_f32, dims):
    cols = rhs_f32.shape[-1]
    parts = lax.dot_general(
        lhs, split3(rhs_f32), (dims, ((), ())), preferred_element_type=jnp.float32
    )
    return parts[:, :cols] + parts[:, cols : 2 * cols] + parts[:, 2 * cols :]


def solve_gains(data, model_re, model_im):
    count = data.shape[0]

    def sweep(gain_re, gain_im):
        probe_re = gain_re * model_re - gain_im * model_im
        probe_im = gain_re * model_im + gain_im * model_re
        power = jnp.sum(probe_re * probe_re + probe_im * probe_im)
        half = exact_dot(data, jnp.stack([probe_re, probe_im], axis=1), ((0,), (0,)))
        u_re = half[:SPECTRA, 0] + half[SPECTRA:, 1]
        u_im = half[:SPECTRA, 1] - half[SPECTRA:, 0]
        mix = jnp.concatenate(
            [jnp.stack([u_re, u_im], axis=1), jnp.stack([-u_im, u_re], axis=1)], axis=0
        )
        product = exact_dot(data, mix, ((1,), (0,))) * (1.0 / SPECTRA)
        product_re = product[:, 0]
        product_im = product[:, 1]
        denominator = (model_re * model_re + model_im * model_im) * (power + 1e-06)
        new_re = (model_re * product_re + model_im * product_im) / denominator
        new_im = (model_re * product_im - model_im * product_re) / denominator
        return new_re, new_im

    def paired(step_index, carried):
        first_re, first_im = sweep(carried[0], carried[1])
        second_re, second_im = sweep(first_re, first_im)
        return (0.5 * (second_re + first_re), 0.5 * (second_im + first_im))

    start_re = jnp.ones((count,), jnp.float32)
    start_im = jnp.zeros((count,), jnp.float32)
    return lax.fori_loop(0, ITERS // 2, paired, (start_re, start_im), unroll=True)


def correlate_kernel(block_ref, rows_ref, cols_ref, out_ref, turned_ref):
    width = rows_ref.shape[-1]
    rows = rows_ref[:, 0].reshape(-1, width)

    @pl.when(pl.program_id(1) == 0)
    def _():
        turned_ref[:, :SPECTRA] = rows[:, SPECTRA:]
        turned_ref[:, SPECTRA:] = -rows[:, :SPECTRA]

    cols = cols_ref[:, 0].reshape(-1, width)
    dims = (((1,), (1,)), ((), ()))
    real = lax.dot_general(rows, cols, dims, preferred_element_type=jnp.float32)
    imag = lax.dot_general(turned_ref[...], cols, dims, preferred_element_type=jnp.float32)
    out_ref[0, 0] = (real * (1.0 / SPECTRA)).astype(out_ref.dtype)
    out_ref[1, 0] = (imag * (1.0 / SPECTRA)).astype(out_ref.dtype)


def correlate_into_kernel(block_ref, rows_ref, cols_ref, prev_ref, out_ref, turned_ref):
    correlate_kernel(block_ref, rows_ref, cols_ref, out_ref, turned_ref)


def correlate(data, scalars, row_count, out=None, total_chans=None, col_block=1024):
    devices, chans, per, width = data.shape
    inputs = devices * per
    total_chans = chans if total_chans is None else total_chans
    grid = (chans, inputs // col_block)
    row_devices = row_count // per
    col_devices = col_block // per
    in_specs = [
        pl.BlockSpec((row_devices, 1, per, width), lambda c, j, s: (s[0], c, 0, 0)),
        pl.BlockSpec((col_devices, 1, per, width), lambda c, j, s: (j, c, 0, 0)),
    ]
    operands = [scalars, data, data]
    aliases = {}
    if out is not None:
        in_specs.append(pl.BlockSpec(memory_space=pl.ANY))
        operands.append(out)
        aliases = {3: 0}
    spec = pltpu.PrefetchScalarGridSpec(
        num_scalar_prefetch=1,
        grid=grid,
        in_specs=in_specs,
        out_specs=pl.BlockSpec((2, 1, row_count, col_block), lambda c, j, s: (0, s[1] + c, 0, j)),
        scratch_shapes=[pltpu.VMEM((row_count, width), data.dtype)],
    )
    flops = 8 * chans * row_count * inputs * (width // 2)
    kernel = correlate_kernel if out is None else correlate_into_kernel
    return pl.pallas_call(
        kernel,
        grid_spec=spec,
        out_shape=jax.ShapeDtypeStruct((2, total_chans, row_count, inputs), jnp.bfloat16),
        input_output_aliases=aliases,
        cost_estimate=pl.CostEstimate(
            flops=flops,
            transcendentals=0,
            bytes_accessed=2 * chans * (inputs * width + row_count * width + 2 * row_count * inputs),
        ),
    )(*operands)


def shards(voltages, flags, model_amp, model_phase):
    keep = (1 - flags).astype(jnp.float32)
    input_count = voltages.shape[0]
    spectra = channelize(voltages, keep)
    blk_count = lax.axis_size("blk")
    chan_count = lax.axis_size("chan")
    block_index = lax.axis_index("blk")
    spectra = spectra.reshape(chan_count, 2, 2, input_count, 2 * SPECTRA)
    first_send = spectra
    second_send = spectra[:, ::-1]
    devices = chan_count * blk_count

    def turn(send):
        send = send.reshape(devices, input_count, 2 * SPECTRA)
        return lax.all_to_all(send, ("chan", "blk"), split_axis=0, concat_axis=0, tiled=True)

    own = turn(first_send)
    all_inputs = devices * input_count
    row_count = all_inputs // blk_count
    core = block_index % 2
    level = block_index // 2
    swap = [(b, b ^ 1) for b in range(blk_count)]
    own_partner = lax.ppermute(own, "blk", perm=swap)

    solve = 2 * core + level
    amp = lax.dynamic_index_in_dim(model_amp, solve, 0, keepdims=False)
    phase = lax.dynamic_index_in_dim(model_phase, solve, 0, keepdims=False)
    full_re = amp * jnp.cos(phase)
    full_im = amp * jnp.sin(phase)
    other = turn(second_send)
    other_partner = lax.ppermute(other, "blk", perm=swap)
    local_chans = 4
    shape = (devices, 1, input_count, 2 * SPECTRA)

    def correlate_into(visibility, data, chan):
        scalars = jnp.stack([block_index, chan]).astype(jnp.int32)
        return correlate(
            data.reshape(shape), scalars, row_count, out=visibility, total_chans=local_chans
        )

    solved = jnp.stack(solve_gains(own.reshape(all_inputs, -1), full_re, full_im))
    owners = solved.reshape(2, devices, 1, input_count)
    gains = lax.all_to_all(owners, ("chan", "blk"), split_axis=1, concat_axis=1, tiled=True)
    gains = gains.reshape(2, chan_count, 2, 2, input_count)
    gains = jnp.swapaxes(gains, 2, 3).reshape(2, -1, input_count)

    visibility = None
    for data, chan in (
        (own, 2 * core + level),
        (other, 2 * core + 1 - level),
        (own_partner, 2 - 2 * core + level),
        (other_partner, 3 - 2 * core - level),
    ):
        visibility = correlate_into(visibility, data, chan)
    return (visibility, gains)


def solution(mesh):
    return jax.shard_map(
        shards,
        mesh=mesh,
        in_specs=(P(("chan", "blk"), None), P(("chan", "blk")), P("chan", None), P("chan", None)),
        out_specs=(P(None, "chan", "blk", None), P(None, None, ("chan", "blk"))),
        check_vma=False,
    )
```

```python
import math

import jax
import jax.numpy as jnp
from jax import lax
from jax.experimental import pallas as pl
from jax.experimental.pallas import tpu as pltpu
from jax.sharding import PartitionSpec as P

CHANS = 128
FRAME = 512
TAPS = 8
BAND_START = 64
SPECTRA = 256
ITERS = 10


def window_table():
    index = jnp.arange(TAPS * FRAME, dtype=jnp.float32)
    offset = (index - TAPS * FRAME / 2 + 0.5) / FRAME
    taper = 0.5 - 0.5 * jnp.cos(2.0 * math.pi * (index + 0.5) / (TAPS * FRAME))
    return (jnp.sinc(offset) * taper).reshape(TAPS, FRAME)


def transform_table():
    sample = jnp.arange(FRAME, dtype=jnp.int32)
    channel = BAND_START + jnp.arange(CHANS, dtype=jnp.int32)
    angle = (sample[:, None] * channel[None, :] % FRAME).astype(jnp.float32) * (
        2.0 * math.pi / FRAME
    )
    return jnp.stack([jnp.cos(angle), -jnp.sin(angle)], axis=1).astype(jnp.bfloat16)


def transform_kernel(keep_ref, window_ref, table_ref, samples_ref, out_ref, wide_ref):
    group = samples_ref.shape[0]
    base = pl.program_id(0) * group
    scale = 1.0 / (64.0 * math.sqrt(FRAME))
    for item in range(group):
        wide_ref[0 : SPECTRA + TAPS - 1, :] = samples_ref[item].astype(jnp.float32)
        frames = window_ref[0:1, :] * wide_ref[0:SPECTRA, :]
        for tap in range(1, TAPS):
            frames = frames + window_ref[tap : tap + 1, :] * wide_ref[tap : tap + SPECTRA, :]
        result = lax.dot_general(
            table_ref[...], frames.astype(jnp.bfloat16), (((1,), (1,)), ((), ())),
            preferred_element_type=jnp.float32,
        )
        result = result * (scale * keep_ref[base + item])
        out_ref[:, item, :SPECTRA] = result[:CHANS].astype(out_ref.dtype)
        out_ref[:, item, SPECTRA:] = result[CHANS:].astype(out_ref.dtype)


def channelize(voltages, keep):
    window = window_table()
    table = transform_table()
    count = voltages.shape[0]
    samples = voltages.reshape(count, SPECTRA + TAPS - 1, FRAME)
    order = jnp.arange(CHANS).reshape(-1, 2, 2).transpose(0, 2, 1).reshape(-1)
    table_t = jnp.transpose(table[:, :, order].reshape(FRAME, 2 * CHANS))
    group = 8
    return pl.pallas_call(
        transform_kernel,
        grid=(count // group,),
        in_specs=[
            pl.BlockSpec(memory_space=pltpu.SMEM),
            pl.BlockSpec((TAPS, FRAME), lambda g: (0, 0)),
            pl.BlockSpec((2 * CHANS, FRAME), lambda g: (0, 0)),
            pl.BlockSpec((group, SPECTRA + TAPS - 1, FRAME), lambda g: (g, 0, 0)),
        ],
        out_specs=pl.BlockSpec((CHANS, group, 2 * SPECTRA), lambda g: (0, g, 0)),
        out_shape=jax.ShapeDtypeStruct((CHANS, count, 2 * SPECTRA), jnp.bfloat16),
        scratch_shapes=[pltpu.VMEM((SPECTRA + 2 * TAPS, FRAME), jnp.float32)],
        cost_estimate=pl.CostEstimate(
            flops=2 * count * SPECTRA * FRAME * (2 * CHANS + TAPS),
            transcendentals=0,
            bytes_accessed=4 * count * (SPECTRA + TAPS) * FRAME + 2 * CHANS * count * 2 * SPECTRA,
        ),
    )(keep, window, table_t, samples)


def split3(value):
    high = value.astype(jnp.bfloat16)
    rest = value - high.astype(jnp.float32)
    mid = rest.astype(jnp.bfloat16)
    low = (rest - mid.astype(jnp.float32)).astype(jnp.bfloat16)
    return jnp.concatenate([high, mid, low], axis=-1)


def exact_dot(lhs, rhs_f32, dims):
    cols = rhs_f32.shape[-1]
    parts = lax.dot_general(
        lhs, split3(rhs_f32), (dims, ((), ())), preferred_element_type=jnp.float32
    )
    return parts[:, :cols] + parts[:, cols : 2 * cols] + parts[:, 2 * cols :]


def solve_gains(data, model_re, model_im):
    count = data.shape[0]

    def sweep(gain_re, gain_im):
        probe_re = gain_re * model_re - gain_im * model_im
        probe_im = gain_re * model_im + gain_im * model_re
        power = jnp.sum(probe_re * probe_re + probe_im * probe_im)
        half = exact_dot(data, jnp.stack([probe_re, probe_im], axis=1), ((0,), (0,)))
        u_re = half[:SPECTRA, 0] + half[SPECTRA:, 1]
        u_im = half[:SPECTRA, 1] - half[SPECTRA:, 0]
        mix = jnp.concatenate(
            [jnp.stack([u_re, u_im], axis=1), jnp.stack([-u_im, u_re], axis=1)], axis=0
        )
        product = exact_dot(data, mix, ((1,), (0,))) * (1.0 / SPECTRA)
        product_re = product[:, 0]
        product_im = product[:, 1]
        denominator = (model_re * model_re + model_im * model_im) * (power + 1e-06)
        new_re = (model_re * product_re + model_im * product_im) / denominator
        new_im = (model_re * product_im - model_im * product_re) / denominator
        return new_re, new_im

    def paired(step_index, carried):
        first_re, first_im = sweep(carried[0], carried[1])
        second_re, second_im = sweep(first_re, first_im)
        return (0.5 * (second_re + first_re), 0.5 * (second_im + first_im))

    start_re = jnp.ones((count,), jnp.float32)
    start_im = jnp.zeros((count,), jnp.float32)
    return lax.fori_loop(0, ITERS // 2, paired, (start_re, start_im), unroll=True)


def correlate_kernel(block_ref, rows_ref, cols_ref, out_ref, turned_ref):
    width = rows_ref.shape[-1]
    rows = rows_ref[:, 0].reshape(-1, width)

    @pl.when(pl.program_id(1) == 0)
    def _():
        turned_ref[:, :SPECTRA] = rows[:, SPECTRA:]
        turned_ref[:, SPECTRA:] = -rows[:, :SPECTRA]

    cols = cols_ref[:, 0].reshape(-1, width)
    dims = (((1,), (1,)), ((), ()))
    real = lax.dot_general(rows, cols, dims, preferred_element_type=jnp.float32)
    imag = lax.dot_general(turned_ref[...], cols, dims, preferred_element_type=jnp.float32)
    out_ref[0, 0] = (real * (1.0 / SPECTRA)).astype(out_ref.dtype)
    out_ref[1, 0] = (imag * (1.0 / SPECTRA)).astype(out_ref.dtype)


def correlate_into_kernel(block_ref, rows_ref, cols_ref, prev_ref, out_ref, turned_ref):
    correlate_kernel(block_ref, rows_ref, cols_ref, out_ref, turned_ref)


def correlate(data, scalars, row_count, out=None, total_chans=None, col_block=1024):
    devices, chans, per, width = data.shape
    inputs = devices * per
    total_chans = chans if total_chans is None else total_chans
    grid = (chans, inputs // col_block)
    row_devices = row_count // per
    col_devices = col_block // per
    in_specs = [
        pl.BlockSpec((row_devices, 1, per, width), lambda c, j, s: (s[0], c, 0, 0)),
        pl.BlockSpec((col_devices, 1, per, width), lambda c, j, s: (j, c, 0, 0)),
    ]
    operands = [scalars, data, data]
    aliases = {}
    if out is not None:
        in_specs.append(pl.BlockSpec(memory_space=pl.ANY))
        operands.append(out)
        aliases = {3: 0}
    spec = pltpu.PrefetchScalarGridSpec(
        num_scalar_prefetch=1,
        grid=grid,
        in_specs=in_specs,
        out_specs=pl.BlockSpec((2, 1, row_count, col_block), lambda c, j, s: (0, s[1] + c, 0, j)),
        scratch_shapes=[pltpu.VMEM((row_count, width), data.dtype)],
    )
    flops = 8 * chans * row_count * inputs * (width // 2)
    kernel = correlate_kernel if out is None else correlate_into_kernel
    return pl.pallas_call(
        kernel,
        grid_spec=spec,
        out_shape=jax.ShapeDtypeStruct((2, total_chans, row_count, inputs), jnp.bfloat16),
        input_output_aliases=aliases,
        cost_estimate=pl.CostEstimate(
            flops=flops,
            transcendentals=0,
            bytes_accessed=2 * chans * (inputs * width + row_count * width + 2 * row_count * inputs),
        ),
    )(*operands)


def shards(voltages, flags, model_amp, model_phase):
    keep = (1 - flags).astype(jnp.float32)
    input_count = voltages.shape[0]
    spectra = channelize(voltages, keep)
    blk_count = lax.axis_size("blk")
    chan_count = lax.axis_size("chan")
    block_index = lax.axis_index("blk")
    spectra = spectra.reshape(chan_count, 2, 2, input_count, 2 * SPECTRA)
    first_send = spectra
    second_send = spectra[:, ::-1]
    devices = chan_count * blk_count

    def turn(send):
        send = send.reshape(devices, input_count, 2 * SPECTRA)
        return lax.all_to_all(send, ("chan", "blk"), split_axis=0, concat_axis=0, tiled=True)

    own = turn(first_send)
    all_inputs = devices * input_count
    row_count = all_inputs // blk_count
    core = block_index % 2
    level = block_index // 2
    swap = [(b, b ^ 1) for b in range(blk_count)]
    own_partner = lax.ppermute(own, "blk", perm=swap)

    solve = 2 * core + level
    amp = lax.dynamic_index_in_dim(model_amp, solve, 0, keepdims=False)
    phase = lax.dynamic_index_in_dim(model_phase, solve, 0, keepdims=False)
    full_re = amp * jnp.cos(phase)
    full_im = amp * jnp.sin(phase)
    other = turn(second_send)
    other_partner = lax.ppermute(other, "blk", perm=swap)
    local_chans = 4
    shape = (devices, 1, input_count, 2 * SPECTRA)

    def correlate_into(visibility, data, chan):
        scalars = jnp.stack([block_index, chan]).astype(jnp.int32)
        return correlate(
            data.reshape(shape), scalars, row_count, out=visibility, total_chans=local_chans
        )

    solved = jnp.stack(solve_gains(own.reshape(all_inputs, -1), full_re, full_im))
    owners = solved.reshape(2, devices, 1, input_count)
    first = correlate_into(None, own, 2 * core + level)
    owners, first = lax.optimization_barrier((owners, first))
    gains = lax.all_to_all(owners, ("chan", "blk"), split_axis=1, concat_axis=1, tiled=True)
    gains = gains.reshape(2, chan_count, 2, 2, input_count)
    gains = jnp.swapaxes(gains, 2, 3).reshape(2, -1, input_count)

    visibility = first
    for data, chan in (
        (other, 2 * core + 1 - level),
        (own_partner, 2 - 2 * core + level),
        (other_partner, 3 - 2 * core - level),
    ):
        visibility = correlate_into(visibility, data, chan)
    return (visibility, gains)


def solution(mesh):
    return jax.shard_map(
        shards,
        mesh=mesh,
        in_specs=(P(("chan", "blk"), None), P(("chan", "blk")), P("chan", None), P("chan", None)),
        out_specs=(P(None, "chan", "blk", None), P(None, None, ("chan", "blk"))),
        check_vma=False,
    )
```
